512 devices in a mesh: lon: 32 (over y_hi, x, core), lat: 16 (over z, y_lo).
Axes of the slice: x: 4, y: 8 (y_hi: 4, y_lo: 2; y = y_hi * 2 + y_lo), z: 8, core: 2. Of those that a mesh axis runs over, the one named last changes fastest.
Arguments:
- latent_frame: bfloat16 [256, 2048, 128], P('lat', 'lon'), may hold values from -6 to 6
- weights_in: bfloat16 [3, 3, 128, 128], replicated, may hold values from -0.1875 to 0.1875
- weights_out: bfloat16 [3, 3, 128, 128], replicated, may hold values from -0.1875 to 0.1875
- cotangent: bfloat16 [256, 2048, 128], P('lat', 'lon'), may hold values from -0.0059814453 to 0.0059814453
Outputs:
- decoded: bfloat16 [256, 2048, 128], P('lat', 'lon')
- grad_weights_in: float32 [3, 3, 128, 128], replicated
- grad_weights_out: float32 [3, 3, 128, 128], replicated
The draws below stay inside these ranges and needn't reach their ends.
All inputs are finite; a program needn't handle non-finite values.
Results may differ from the reference program's by a relative error of at most 0.0049.
Values may be sent and summed in bfloat16 or wider, within the bound.
No kernel may reach another device: no remote copies, remote signals or barrier semaphores. Data moves between devices by JAX's collectives and lax.ppermute only.
A program may use at most 64 MiB of HBM per device.

```python
import jax
import jax.numpy as jnp
from jax import lax

C = 128
TILE_LAT = 16
LAT = 256
LON = 2048
N_LAT = 16


def block_levels(rng, extent, cuts, low, top_value):
    def one(dim, parts):
        heights = jax.random.uniform(jax.random.fold_in(jax.random.fold_in(rng, 6), dim), (parts,), jnp.float32, low / len(cuts), top_value / len(cuts))
        return jnp.repeat(jnp.exp(heights), extent[dim] // parts).reshape((-1,) + (1,) * (len(extent) - dim - 1))

    level = one(*cuts[0])
    for cut in cuts[1:]:
        level = level * one(*cut)
    return level


def bell_draw(own_key, extent, width, bound, cuts=(), kind=jnp.bfloat16):
    result = jax.random.normal(own_key, extent, jnp.float32) * width
    if len(cuts) > 0:
        result = block_levels(own_key, extent, cuts, -0.22, 0.18) * result
    return jnp.clip(result, min=-bound, max=bound).astype(kind)


def setup_inputs(seed: int = 0) -> dict:
    keys = jax.random.split(jax.random.key(seed), 5)
    latent_frame = bell_draw(keys[0], (LAT, LON, C), 1.0, 6.0, ((0, 16), (1, 32)))
    weights_in = bell_draw(keys[1], (3, 3, C, C), (9 * C) ** -0.5, 0.1875)
    weights_out = bell_draw(keys[2], (3, 3, C, C), (9 * C) ** -0.5, 0.1875)
    cotangent = bell_draw(keys[3], (LAT, LON, C), 0.001, 0.0059814453, ((0, 16), (1, 32)))
    return {"latent_frame": latent_frame, "weights_in": weights_in, "weights_out": weights_out, "cotangent": cotangent}


def pad_cycle(field):
    wrapped = jnp.pad(field, ((0, 0), (1, 1), (0, 0)), mode="wrap")
    return jnp.pad(wrapped, ((1, 1), (0, 0), (0, 0)))


def conv_tile(padded, weights):
    rows_out = padded.shape[0] - 2
    cols_out = padded.shape[1] - 2
    channels = padded.shape[2]
    summed = jnp.zeros((rows_out * cols_out, weights.shape[3]), jnp.float32)
    for row_tap in range(3):
        for col_tap in range(3):
            window = padded[row_tap:row_tap + rows_out, col_tap:col_tap + cols_out].reshape(rows_out * cols_out, channels)
            summed = summed + jnp.dot(window, weights[row_tap, col_tap], preferred_element_type=jnp.float32)
    return summed.reshape(rows_out, cols_out, weights.shape[3])


def weight_terms(padded, gradient):
    rows_out, cols_out, channels = gradient.shape
    flat_grad = gradient.reshape(rows_out * cols_out, channels)
    taps = []
    for row_tap in range(3):
        for col_tap in range(3):
            window = padded[row_tap:row_tap + rows_out, col_tap:col_tap + cols_out].reshape(rows_out * cols_out, padded.shape[2])
            taps.append(lax.dot_general(window, flat_grad, (((0,), (0,)), ((), ())), preferred_element_type=jnp.float32))
    return jnp.stack(taps).reshape(3, 3, padded.shape[2], channels)


def reference(latent_frame, weights_in, weights_out, cotangent):
    padded_input = pad_cycle(latent_frame)
    padded_grad = pad_cycle(cotangent)
    band_ids = jnp.arange(N_LAT, dtype=jnp.int32)

    def hidden_band(index):
        band_rows = lax.dynamic_slice_in_dim(padded_input, index * TILE_LAT, TILE_LAT + 2, 0)
        return jax.nn.silu(conv_tile(band_rows, weights_in)).astype(jnp.bfloat16)

    hidden = lax.map(hidden_band, band_ids).reshape(LAT, LON, C)
    padded_hidden = pad_cycle(hidden)
    flipped = jnp.transpose(weights_out[::-1, ::-1], (0, 1, 3, 2))

    def band_step(totals, index):
        input_rows = lax.dynamic_slice_in_dim(padded_input, index * TILE_LAT, TILE_LAT + 2, 0)
        hidden_rows = lax.dynamic_slice_in_dim(padded_hidden, index * TILE_LAT, TILE_LAT + 2, 0)
        grad_rows = lax.dynamic_slice_in_dim(padded_grad, index * TILE_LAT, TILE_LAT + 2, 0)
        preact = conv_tile(input_rows, weights_in)
        output = conv_tile(hidden_rows, weights_out).astype(jnp.bfloat16)
        inner_grad = grad_rows[1:-1, 1:-1]
        term_out = weight_terms(hidden_rows, inner_grad)
        grad_hidden = conv_tile(grad_rows, flipped)
        sigmoid_pre = jax.nn.sigmoid(preact)
        grad_pre = (grad_hidden * (sigmoid_pre * (1.0 + preact * (1.0 - sigmoid_pre)))).astype(jnp.bfloat16)
        term_in = weight_terms(input_rows, grad_pre)
        return (totals[0] + term_in, totals[1] + term_out), output

    zeros = jnp.zeros((3, 3, C, C), jnp.float32)
    (grad_in, grad_out), outputs = lax.scan(band_step, (zeros, zeros), band_ids)
    return outputs.reshape(LAT, LON, C), grad_in, grad_out
```

```python
import jax
import jax.numpy as jnp
from jax import lax
from jax.sharding import PartitionSpec as P


def with_halo(block, sides, width, periodic):
    for axis, dim in sides:
        count = lax.axis_size(axis)
        forward = [(i, i + 1) for i in range(count - 1)]
        if periodic:
            forward.append((count - 1, 0))
        backward = [(target, source) for source, target in forward]
        low = lax.ppermute(
            lax.slice_in_dim(block, block.shape[dim] - width, None, axis=dim), axis, forward
        )
        high = lax.ppermute(lax.slice_in_dim(block, 0, width, axis=dim), axis, backward)
        block = jnp.concatenate([low, block, high], axis=dim)
    return block


def in_blocks(x, dim, devices):
    dims = x.shape
    blocks = x.reshape(*dims[:dim], devices, dims[dim] // devices, *dims[dim + 1 :])
    return jnp.moveaxis(blocks, dim, 0)


def sent_and_summed(x, axis, dim):
    blocks = in_blocks(x, dim, lax.axis_size(axis))
    arrived = lax.all_to_all(blocks, axis, split_axis=0, concat_axis=0, tiled=True)
    return arrived.sum(axis=0)


def sent_to_all(x, axis):
    copies = jnp.broadcast_to(x, (lax.axis_size(axis), *x.shape))
    return lax.all_to_all(copies, axis, split_axis=0, concat_axis=0, tiled=True)


def taken_together(x, axis):
    everything = sent_to_all(x, axis)
    return jnp.sum(everything, axis=0)


def in_order(blocks, dim):
    blocks = jnp.moveaxis(blocks, 0, dim)
    dims = blocks.shape
    return blocks.reshape(*dims[:dim], dims[dim] * dims[dim + 1], *dims[dim + 2 :])


def collect(x, axis, dim):
    return in_order(sent_to_all(x, axis), dim)


def conv_tile(padded, weights):
    rows_out = padded.shape[0] - 2
    cols_out = padded.shape[1] - 2
    channels = padded.shape[2]
    summed = jnp.zeros((rows_out * cols_out, weights.shape[3]), jnp.float32)
    for row_tap in range(3):
        for col_tap in range(3):
            window = padded[row_tap : row_tap + rows_out, col_tap : col_tap + cols_out].reshape(
                rows_out * cols_out, channels
            )
            summed = summed + jnp.dot(
                window, weights[row_tap, col_tap], preferred_element_type=jnp.float32
            )
    return summed.reshape(rows_out, cols_out, weights.shape[3])


def weight_terms(padded, gradient):
    rows_out, cols_out, channels = gradient.shape
    flat_grad = gradient.reshape(rows_out * cols_out, channels)
    taps = []
    for row_tap in range(3):
        for col_tap in range(3):
            window = padded[row_tap : row_tap + rows_out, col_tap : col_tap + cols_out].reshape(
                rows_out * cols_out, padded.shape[2]
            )
            taps.append(
                lax.dot_general(
                    window, flat_grad, (((0,), (0,)), ((), ())), preferred_element_type=jnp.float32
                )
            )
    return jnp.stack(taps).reshape(3, 3, padded.shape[2], channels)


def shards(latent_frame, weights_in, weights_out, cotangent):
    tile_rows = latent_frame.shape[0]
    channels = latent_frame.shape[2]
    stacked = jnp.stack([latent_frame, cotangent])
    margin = 2
    widened = with_halo(stacked, (("lon", 2),), margin, True)
    extended = with_halo(widened, (("lat", 1),), margin, False)
    input_pad = extended[0]
    grad_pad = extended[1][1:-1, 1:-1]
    preact_wide = conv_tile(input_pad, weights_in)
    hidden_wide = jax.nn.silu(preact_wide).astype(jnp.bfloat16)
    global_row = lax.axis_index("lat") * tile_rows - 1 + jnp.arange(tile_rows + 2, dtype=jnp.int32)
    inside = (global_row >= 0) & (global_row < tile_rows * lax.axis_size("lat"))
    hidden_pad = jnp.where(inside[:, None, None], hidden_wide, jnp.zeros_like(hidden_wide))
    preact = preact_wide[1:-1, 1:-1]
    input_use = input_pad[1:-1, 1:-1]
    decoded = conv_tile(hidden_pad, weights_out).astype(jnp.bfloat16)
    term_out = weight_terms(hidden_pad, cotangent)
    flipped = jnp.transpose(weights_out[::-1, ::-1], (0, 1, 3, 2))
    grad_hidden = conv_tile(grad_pad, flipped)
    sigmoid_pre = jax.nn.sigmoid(preact)
    grad_pre = (grad_hidden * (sigmoid_pre * (1.0 + preact * (1.0 - sigmoid_pre)))).astype(
        jnp.bfloat16
    )
    term_in = weight_terms(input_use, grad_pre)
    all_terms = jnp.concatenate(
        [term_in.reshape(9 * channels, channels), term_out.reshape(9 * channels, channels)], axis=0
    )
    summed = lax.psum(all_terms, ("lon", "lat"))
    grad_in = summed[: 9 * channels].reshape(3, 3, channels, channels)
    grad_out = summed[9 * channels :].reshape(3, 3, channels, channels)
    return (decoded, grad_in, grad_out)


def solution(mesh):
    placed = (P("lat", "lon", None), P(), P(), P("lat", "lon", None))
    return jax.shard_map(
        shards,
        mesh=mesh,
        in_specs=placed,
        out_specs=(P("lat", "lon", None), P(), P()),
        check_vma=False,
    )
```

```python
import jax
import jax.numpy as jnp
from jax import lax
from jax.sharding import PartitionSpec as P


def neighbour_pairs(count, step, periodic):
    pairs = []
    for source in range(count):
        target = source + step
        if periodic:
            target %= count
        if 0 <= target < count:
            pairs.append((source, target))
    return pairs


def from_neighbours(piece, lat_step, lon_step):
    n_lat, n_lon = lax.axis_size("lat"), lax.axis_size("lon")
    if lat_step == 0:
        return lax.ppermute(piece, "lon", neighbour_pairs(n_lon, lon_step, True))
    if lon_step == 0:
        return lax.ppermute(piece, "lat", neighbour_pairs(n_lat, lat_step, False))
    pairs = []
    for lat_source, lat_target in neighbour_pairs(n_lat, lat_step, False):
        for lon_source, lon_target in neighbour_pairs(n_lon, lon_step, True):
            pairs.append((lon_source * n_lat + lat_source, lon_target * n_lat + lat_target))
    return lax.ppermute(piece, ("lon", "lat"), pairs)


def with_halo(block, width):
    rows, cols = block.shape[1], block.shape[2]
    top, bottom = slice(rows - width, rows), slice(0, width)
    left, right = slice(cols - width, cols), slice(0, width)
    every = slice(None)
    received = {}
    for lat_step, row_part in ((1, top), (0, every), (-1, bottom)):
        for lon_step, col_part in ((1, left), (0, every), (-1, right)):
            if lat_step == 0 and lon_step == 0:
                continue
            received[lat_step, lon_step] = from_neighbours(
                block[:, row_part, col_part], lat_step, lon_step
            )
    received[0, 0] = block
    bands = [
        jnp.concatenate([received[lat_step, 1], received[lat_step, 0], received[lat_step, -1]], axis=2)
        for lat_step in (1, 0, -1)
    ]
    return jnp.concatenate(bands, axis=1)


def in_blocks(x, dim, devices):
    dims = x.shape
    blocks = x.reshape(*dims[:dim], devices, dims[dim] // devices, *dims[dim + 1 :])
    return jnp.moveaxis(blocks, dim, 0)


def sent_and_summed(x, axis, dim):
    blocks = in_blocks(x, dim, lax.axis_size(axis))
    arrived = lax.all_to_all(blocks, axis, split_axis=0, concat_axis=0, tiled=True)
    return arrived.sum(axis=0)


def sent_to_all(x, axis):
    copies = jnp.broadcast_to(x, (lax.axis_size(axis), *x.shape))
    return lax.all_to_all(copies, axis, split_axis=0, concat_axis=0, tiled=True)


def taken_together(x, axis):
    everything = sent_to_all(x, axis)
    return jnp.sum(everything, axis=0)


def in_order(blocks, dim):
    blocks = jnp.moveaxis(blocks, 0, dim)
    dims = blocks.shape
    return blocks.reshape(*dims[:dim], dims[dim] * dims[dim + 1], *dims[dim + 2 :])


def collect(x, axis, dim):
    return in_order(sent_to_all(x, axis), dim)


def windows(padded, rows_out, cols_out):
    taps = [
        padded[row_tap : row_tap + rows_out, col_tap : col_tap + cols_out]
        for row_tap in range(3)
        for col_tap in range(3)
    ]
    return jnp.concatenate(taps, axis=-1).reshape(rows_out * cols_out, 9 * padded.shape[2])


def conv_tile(padded, weights):
    rows_out = padded.shape[0] - 2
    cols_out = padded.shape[1] - 2
    stacked = windows(padded, rows_out, cols_out)
    summed = jnp.dot(
        stacked, weights.reshape(-1, weights.shape[3]), preferred_element_type=jnp.float32
    )
    return summed.reshape(rows_out, cols_out, weights.shape[3])


def weight_terms(padded, gradient):
    rows_out, cols_out, channels = gradient.shape
    flat_grad = gradient.reshape(rows_out * cols_out, channels)
    stacked = windows(padded, rows_out, cols_out)
    terms = lax.dot_general(
        stacked, flat_grad, (((0,), (0,)), ((), ())), preferred_element_type=jnp.float32
    )
    return terms.reshape(3, 3, padded.shape[2], channels)


def shards(latent_frame, weights_in, weights_out, cotangent):
    tile_rows = latent_frame.shape[0]
    channels = latent_frame.shape[2]
    stacked = jnp.stack([latent_frame, cotangent])
    margin = 2
    extended = with_halo(stacked, margin)
    input_pad = extended[0]
    grad_pad = extended[1][1:-1, 1:-1]
    preact_wide = conv_tile(input_pad, weights_in)
    hidden_wide = jax.nn.silu(preact_wide).astype(jnp.bfloat16)
    global_row = lax.axis_index("lat") * tile_rows - 1 + jnp.arange(tile_rows + 2, dtype=jnp.int32)
    inside = (global_row >= 0) & (global_row < tile_rows * lax.axis_size("lat"))
    hidden_pad = jnp.where(inside[:, None, None], hidden_wide, jnp.zeros_like(hidden_wide))
    preact = preact_wide[1:-1, 1:-1]
    input_use = input_pad[1:-1, 1:-1]
    decoded = conv_tile(hidden_pad, weights_out).astype(jnp.bfloat16)
    term_out = weight_terms(hidden_pad, cotangent)
    flipped = jnp.transpose(weights_out[::-1, ::-1], (0, 1, 3, 2))
    grad_hidden = conv_tile(grad_pad, flipped)
    sigmoid_pre = jax.nn.sigmoid(preact)
    grad_pre = (grad_hidden * (sigmoid_pre * (1.0 + preact * (1.0 - sigmoid_pre)))).astype(
        jnp.bfloat16
    )
    term_in = weight_terms(input_use, grad_pre)
    all_terms = jnp.concatenate(
        [term_in.reshape(9 * channels, channels), term_out.reshape(9 * channels, channels)], axis=0
    )
    portion = sent_and_summed(all_terms, "lon", 0)
    portion = taken_together(portion, "lat")
    summed = collect(portion, "lon", 0)
    grad_in = summed[: 9 * channels].reshape(3, 3, channels, channels)
    grad_out = summed[9 * channels :].reshape(3, 3, channels, channels)
    return (decoded, grad_in, grad_out)


def solution(mesh):
    placed = (P("lat", "lon", None), P(), P(), P("lat", "lon", None))
    return jax.shard_map(
        shards,
        mesh=mesh,
        in_specs=placed,
        out_specs=(P("lat", "lon", None), P(), P()),
        check_vma=False,
    )
```

```python
import jax
import jax.numpy as jnp
from jax import lax
from jax.sharding import PartitionSpec as P


def with_halo(block, sides, width, periodic):
    for axis, dim in sides:
        count = lax.axis_size(axis)
        forward = [(i, i + 1) for i in range(count - 1)]
        if periodic:
            forward.append((count - 1, 0))
        backward = [(target, source) for source, target in forward]
        low = lax.ppermute(
            lax.slice_in_dim(block, block.shape[dim] - width, None, axis=dim), axis, forward
        )
        high = lax.ppermute(lax.slice_in_dim(block, 0, width, axis=dim), axis, backward)
        block = jnp.concatenate([low, block, high], axis=dim)
    return block


def in_blocks(x, dim, devices):
    dims = x.shape
    blocks = x.reshape(*dims[:dim], devices, dims[dim] // devices, *dims[dim + 1 :])
    return jnp.moveaxis(blocks, dim, 0)


def sent_and_summed(x, axis, dim):
    blocks = in_blocks(x, dim, lax.axis_size(axis))
    arrived = lax.all_to_all(blocks, axis, split_axis=0, concat_axis=0, tiled=True)
    return arrived.sum(axis=0)


def sent_to_all(x, axis):
    copies = jnp.broadcast_to(x, (lax.axis_size(axis), *x.shape))
    return lax.all_to_all(copies, axis, split_axis=0, concat_axis=0, tiled=True)


def taken_together(x, axis):
    everything = sent_to_all(x, axis)
    return jnp.sum(everything, axis=0)


def in_order(blocks, dim):
    blocks = jnp.moveaxis(blocks, 0, dim)
    dims = blocks.shape
    return blocks.reshape(*dims[:dim], dims[dim] * dims[dim + 1], *dims[dim + 2 :])


def collect(x, axis, dim):
    return in_order(sent_to_all(x, axis), dim)


def windows(padded, rows_out, cols_out):
    taps = [
        padded[row_tap : row_tap + rows_out, col_tap : col_tap + cols_out]
        for row_tap in range(3)
        for col_tap in range(3)
    ]
    return jnp.concatenate(taps, axis=-1).reshape(rows_out * cols_out, 9 * padded.shape[2])


def conv_tile(padded, weights):
    rows_out = padded.shape[0] - 2
    cols_out = padded.shape[1] - 2
    stacked = windows(padded, rows_out, cols_out)
    summed = jnp.dot(
        stacked, weights.reshape(-1, weights.shape[3]), preferred_element_type=jnp.float32
    )
    return summed.reshape(rows_out, cols_out, weights.shape[3])


def weight_terms(padded, gradient):
    rows_out, cols_out, channels = gradient.shape
    flat_grad = gradient.reshape(rows_out * cols_out, channels)
    stacked = windows(padded, rows_out, cols_out)
    terms = lax.dot_general(
        stacked, flat_grad, (((0,), (0,)), ((), ())), preferred_element_type=jnp.float32
    )
    return terms.reshape(3, 3, padded.shape[2], channels)


def shards(latent_frame, weights_in, weights_out, cotangent):
    tile_rows = latent_frame.shape[0]
    channels = latent_frame.shape[2]
    stacked = jnp.stack([latent_frame, cotangent])
    margin = 2
    widened = with_halo(stacked, (("lon", 2),), margin, True)
    extended = with_halo(widened, (("lat", 1),), margin, False)
    input_pad = extended[0]
    grad_pad = extended[1][1:-1, 1:-1]
    preact_wide = conv_tile(input_pad, weights_in)
    hidden_wide = jax.nn.silu(preact_wide).astype(jnp.bfloat16)
    global_row = lax.axis_index("lat") * tile_rows - 1 + jnp.arange(tile_rows + 2, dtype=jnp.int32)
    inside = (global_row >= 0) & (global_row < tile_rows * lax.axis_size("lat"))
    hidden_pad = jnp.where(inside[:, None, None], hidden_wide, jnp.zeros_like(hidden_wide))
    preact = preact_wide[1:-1, 1:-1]
    input_use = input_pad[1:-1, 1:-1]
    decoded = conv_tile(hidden_pad, weights_out).astype(jnp.bfloat16)
    term_out = weight_terms(hidden_pad, cotangent)
    flipped = jnp.transpose(weights_out[::-1, ::-1], (0, 1, 3, 2))
    grad_hidden = conv_tile(grad_pad, flipped)
    sigmoid_pre = jax.nn.sigmoid(preact)
    grad_pre = (grad_hidden * (sigmoid_pre * (1.0 + preact * (1.0 - sigmoid_pre)))).astype(
        jnp.bfloat16
    )
    term_in = weight_terms(input_use, grad_pre)
    all_terms = jnp.concatenate(
        [term_in.reshape(9 * channels, channels), term_out.reshape(9 * channels, channels)], axis=0
    )
    portion = sent_and_summed(all_terms, "lon", 0)
    portion = taken_together(portion, "lat")
    summed = collect(portion, "lon", 0)
    grad_in = summed[: 9 * channels].reshape(3, 3, channels, channels)
    grad_out = summed[9 * channels :].reshape(3, 3, channels, channels)
    return (decoded, grad_in, grad_out)


def solution(mesh):
    placed = (P("lat", "lon", None), P(), P(), P("lat", "lon", None))
    return jax.shard_map(
        shards,
        mesh=mesh,
        in_specs=placed,
        out_specs=(P("lat", "lon", None), P(), P()),
        check_vma=False,
    )
```

```python
import jax
import jax.numpy as jnp
from jax import lax
from jax.sharding import Mesh, PartitionSpec as P

LON = ("lon_chip", "core")


def with_halo(block, sides, width, periodic):
    for axis, dim in sides:
        count = lax.axis_size(axis)
        forward = [(i, i + 1) for i in range(count - 1)]
        if periodic:
            forward.append((count - 1, 0))
        backward = [(target, source) for source, target in forward]
        low = lax.ppermute(
            lax.slice_in_dim(block, block.shape[dim] - width, None, axis=dim), axis, forward
        )
        high = lax.ppermute(lax.slice_in_dim(block, 0, width, axis=dim), axis, backward)
        block = jnp.concatenate([low, block, high], axis=dim)
    return block


def in_blocks(x, dim, devices):
    dims = x.shape
    blocks = x.reshape(*dims[:dim], devices, dims[dim] // devices, *dims[dim + 1 :])
    return jnp.moveaxis(blocks, dim, 0)


def sent_and_summed(x, axis, dim):
    blocks = in_blocks(x, dim, lax.axis_size(axis))
    arrived = lax.all_to_all(blocks, axis, split_axis=0, concat_axis=0, tiled=True)
    return arrived.sum(axis=0)


def sent_to_all(x, axis):
    copies = jnp.broadcast_to(x, (lax.axis_size(axis), *x.shape))
    return lax.all_to_all(copies, axis, split_axis=0, concat_axis=0, tiled=True)


def taken_together(x, axis):
    everything = sent_to_all(x, axis)
    return jnp.sum(everything, axis=0)


def in_order(blocks, dim):
    blocks = jnp.moveaxis(blocks, 0, dim)
    dims = blocks.shape
    return blocks.reshape(*dims[:dim], dims[dim] * dims[dim + 1], *dims[dim + 2 :])


def collect(x, axis, dim):
    return in_order(sent_to_all(x, axis), dim)


def windows(padded, rows_out, cols_out):
    taps = [
        padded[row_tap : row_tap + rows_out, col_tap : col_tap + cols_out]
        for row_tap in range(3)
        for col_tap in range(3)
    ]
    return jnp.concatenate(taps, axis=-1).reshape(rows_out * cols_out, 9 * padded.shape[2])


def conv_tile(padded, weights):
    rows_out = padded.shape[0] - 2
    cols_out = padded.shape[1] - 2
    stacked = windows(padded, rows_out, cols_out)
    summed = jnp.dot(
        stacked, weights.reshape(-1, weights.shape[3]), preferred_element_type=jnp.float32
    )
    return summed.reshape(rows_out, cols_out, weights.shape[3])


def weight_terms(padded, gradient):
    rows_out, cols_out, channels = gradient.shape
    flat_grad = gradient.reshape(rows_out * cols_out, channels)
    stacked = windows(padded, rows_out, cols_out)
    terms = lax.dot_general(
        stacked, flat_grad, (((0,), (0,)), ((), ())), preferred_element_type=jnp.float32
    )
    return terms.reshape(3, 3, padded.shape[2], channels)


def with_partner(x):
    return lax.ppermute(x, "core", [(0, 1), (1, 0)])


def reduced_everywhere(terms):
    core = lax.axis_index("core")
    half = terms.shape[0] // 2
    mine = lax.dynamic_slice_in_dim(terms, core * half, half, 0)
    other = lax.dynamic_slice_in_dim(terms, (1 - core) * half, half, 0)
    chip_sum = mine + with_partner(other)
    portion = sent_and_summed(chip_sum, "lon_chip", 0)
    portion = taken_together(portion, "lat")
    gathered = collect(portion, "lon_chip", 0)
    partner = with_partner(gathered)
    return jnp.where(
        core == 0,
        jnp.concatenate([gathered, partner], axis=0),
        jnp.concatenate([partner, gathered], axis=0),
    )


def shards(latent_frame, weights_in, weights_out, cotangent):
    tile_rows = latent_frame.shape[0]
    channels = latent_frame.shape[2]
    stacked = jnp.stack([latent_frame, cotangent])
    margin = 2
    widened = with_halo(stacked, ((LON, 2),), margin, True)
    extended = with_halo(widened, (("lat", 1),), margin, False)
    input_pad = extended[0]
    grad_pad = extended[1][1:-1, 1:-1]
    preact_wide = conv_tile(input_pad, weights_in)
    hidden_wide = jax.nn.silu(preact_wide).astype(jnp.bfloat16)
    global_row = lax.axis_index("lat") * tile_rows - 1 + jnp.arange(tile_rows + 2, dtype=jnp.int32)
    inside = (global_row >= 0) & (global_row < tile_rows * lax.axis_size("lat"))
    hidden_pad = jnp.where(inside[:, None, None], hidden_wide, jnp.zeros_like(hidden_wide))
    preact = preact_wide[1:-1, 1:-1]
    input_use = input_pad[1:-1, 1:-1]
    decoded = conv_tile(hidden_pad, weights_out).astype(jnp.bfloat16)
    term_out = weight_terms(hidden_pad, cotangent)
    flipped = jnp.transpose(weights_out[::-1, ::-1], (0, 1, 3, 2))
    grad_hidden = conv_tile(grad_pad, flipped)
    sigmoid_pre = jax.nn.sigmoid(preact)
    grad_pre = (grad_hidden * (sigmoid_pre * (1.0 + preact * (1.0 - sigmoid_pre)))).astype(
        jnp.bfloat16
    )
    term_in = weight_terms(input_use, grad_pre)
    all_terms = jnp.concatenate(
        [term_in.reshape(9 * channels, channels), term_out.reshape(9 * channels, channels)], axis=0
    )
    summed = reduced_everywhere(all_terms)
    grad_in = summed[: 9 * channels].reshape(3, 3, channels, channels)
    grad_out = summed[9 * channels :].reshape(3, 3, channels, channels)
    return (decoded, grad_in, grad_out)


def solution(mesh):
    n_lon, n_lat = mesh.shape["lon"], mesh.shape["lat"]
    split = Mesh(mesh.devices.reshape(n_lon // 2, 2, n_lat), (*LON, "lat"))
    tiled = P("lat", LON, None)
    return jax.shard_map(
        shards,
        mesh=split,
        in_specs=(tiled, P(), P(), tiled),
        out_specs=(tiled, P(), P()),
        check_vma=False,
    )
```

```python
import jax
import jax.numpy as jnp
from jax import lax
from jax.sharding import Mesh, PartitionSpec as P

LON = ("lon_chip", "core")


def with_halo(block, sides, width, periodic):
    for axis, dim in sides:
        count = lax.axis_size(axis)
        forward = [(i, i + 1) for i in range(count - 1)]
        if periodic:
            forward.append((count - 1, 0))
        backward = [(target, source) for source, target in forward]
        low = lax.ppermute(
            lax.slice_in_dim(block, block.shape[dim] - width, None, axis=dim), axis, forward
        )
        high = lax.ppermute(lax.slice_in_dim(block, 0, width, axis=dim), axis, backward)
        block = jnp.concatenate([low, block, high], axis=dim)
    return block


def in_blocks(x, dim, devices):
    dims = x.shape
    blocks = x.reshape(*dims[:dim], devices, dims[dim] // devices, *dims[dim + 1 :])
    return jnp.moveaxis(blocks, dim, 0)


def sent_and_summed(x, axis, dim):
    blocks = in_blocks(x, dim, lax.axis_size(axis))
    arrived = lax.all_to_all(blocks, axis, split_axis=0, concat_axis=0, tiled=True)
    return arrived.sum(axis=0)


def sent_to_all(x, axis):
    copies = jnp.broadcast_to(x, (lax.axis_size(axis), *x.shape))
    return lax.all_to_all(copies, axis, split_axis=0, concat_axis=0, tiled=True)


def taken_together(x, axis):
    everything = sent_to_all(x, axis)
    return jnp.sum(everything, axis=0)


def in_order(blocks, dim):
    blocks = jnp.moveaxis(blocks, 0, dim)
    dims = blocks.shape
    return blocks.reshape(*dims[:dim], dims[dim] * dims[dim + 1], *dims[dim + 2 :])


def collect(x, axis, dim):
    return in_order(sent_to_all(x, axis), dim)


def windows(padded, rows_out, cols_out):
    taps = [
        padded[row_tap : row_tap + rows_out, col_tap : col_tap + cols_out]
        for row_tap in range(3)
        for col_tap in range(3)
    ]
    return jnp.concatenate(taps, axis=-1).reshape(rows_out * cols_out, 9 * padded.shape[2])


def conv_tile(padded, weights):
    rows_out = padded.shape[0] - 2
    cols_out = padded.shape[1] - 2
    stacked = windows(padded, rows_out, cols_out)
    summed = jnp.dot(
        stacked, weights.reshape(-1, weights.shape[3]), preferred_element_type=jnp.float32
    )
    return summed.reshape(rows_out, cols_out, weights.shape[3])


def weight_terms(padded, gradient):
    rows_out, cols_out, channels = gradient.shape
    flat_grad = gradient.reshape(rows_out * cols_out, channels)
    stacked = windows(padded, rows_out, cols_out)
    terms = lax.dot_general(
        stacked, flat_grad, (((0,), (0,)), ((), ())), preferred_element_type=jnp.float32
    )
    return terms.reshape(3, 3, padded.shape[2], channels)


def with_partner(x):
    return lax.ppermute(x, "core", [(0, 1), (1, 0)])


def reduced_everywhere(terms):
    core = lax.axis_index("core")
    half = terms.shape[0] // 2
    mine = lax.dynamic_slice_in_dim(terms, core * half, half, 0)
    other = lax.dynamic_slice_in_dim(terms, (1 - core) * half, half, 0)
    chip_sum = mine + with_partner(other)
    portion = sent_and_summed(chip_sum, "lon_chip", 0)
    portion = taken_together(portion, "lat")
    gathered = collect(portion, "lon_chip", 0)
    partner = with_partner(gathered)
    return jnp.where(core == 0, gathered, partner), jnp.where(core == 0, partner, gathered)


def shards(latent_frame, weights_in, weights_out, cotangent):
    tile_rows = latent_frame.shape[0]
    channels = latent_frame.shape[2]
    stacked = jnp.stack([latent_frame, cotangent])
    margin = 2
    widened = with_halo(stacked, ((LON, 2),), margin, True)
    extended = with_halo(widened, (("lat", 1),), margin, False)
    input_pad = extended[0]
    grad_pad = extended[1][1:-1, 1:-1]
    preact_wide = conv_tile(input_pad, weights_in)
    hidden_wide = jax.nn.silu(preact_wide).astype(jnp.bfloat16)
    global_row = lax.axis_index("lat") * tile_rows - 1 + jnp.arange(tile_rows + 2, dtype=jnp.int32)
    inside = (global_row >= 0) & (global_row < tile_rows * lax.axis_size("lat"))
    hidden_pad = jnp.where(inside[:, None, None], hidden_wide, jnp.zeros_like(hidden_wide))
    preact = preact_wide[1:-1, 1:-1]
    input_use = input_pad[1:-1, 1:-1]
    decoded = conv_tile(hidden_pad, weights_out).astype(jnp.bfloat16)
    term_out = weight_terms(hidden_pad, cotangent)
    flipped = jnp.transpose(weights_out[::-1, ::-1], (0, 1, 3, 2))
    grad_hidden = conv_tile(grad_pad, flipped)
    sigmoid_pre = jax.nn.sigmoid(preact)
    grad_pre = (grad_hidden * (sigmoid_pre * (1.0 + preact * (1.0 - sigmoid_pre)))).astype(
        jnp.bfloat16
    )
    grad_pre = lax.optimization_barrier(grad_pre)
    term_in = weight_terms(input_use, grad_pre)
    all_terms = jnp.concatenate(
        [term_in.reshape(9 * channels, channels), term_out.reshape(9 * channels, channels)], axis=0
    )
    grad_in, grad_out = reduced_everywhere(all_terms)
    grad_in = grad_in.reshape(3, 3, channels, channels)
    grad_out = grad_out.reshape(3, 3, channels, channels)
    return (decoded, grad_in, grad_out)


def solution(mesh):
    n_lon, n_lat = mesh.shape["lon"], mesh.shape["lat"]
    split = Mesh(mesh.devices.reshape(n_lon // 2, 2, n_lat), (*LON, "lat"))
    tiled = P("lat", LON, None)
    return jax.shard_map(
        shards,
        mesh=split,
        in_specs=(tiled, P(), P(), tiled),
        out_specs=(tiled, P(), P()),
        check_vma=False,
    )
```

```python
import jax
import jax.numpy as jnp
from jax import lax
from jax.sharding import Mesh, PartitionSpec as P

LON = ("lon_chip", "core")


def with_halo(block, sides, width, periodic):
    for axis, dim in sides:
        count = lax.axis_size(axis)
        forward = [(i, i + 1) for i in range(count - 1)]
        if periodic:
            forward.append((count - 1, 0))
        backward = [(target, source) for source, target in forward]
        low = lax.ppermute(
            lax.slice_in_dim(block, block.shape[dim] - width, None, axis=dim), axis, forward
        )
        high = lax.ppermute(lax.slice_in_dim(block, 0, width, axis=dim), axis, backward)
        block = jnp.concatenate([low, block, high], axis=dim)
    return block


def in_blocks(x, dim, devices):
    dims = x.shape
    blocks = x.reshape(*dims[:dim], devices, dims[dim] // devices, *dims[dim + 1 :])
    return jnp.moveaxis(blocks, dim, 0)


def sent_and_summed(x, axis, dim):
    blocks = in_blocks(x, dim, lax.axis_size(axis))
    arrived = lax.all_to_all(blocks, axis, split_axis=0, concat_axis=0, tiled=True)
    return arrived.sum(axis=0)


def sent_to_all(x, axis):
    copies = jnp.broadcast_to(x, (lax.axis_size(axis), *x.shape))
    return lax.all_to_all(copies, axis, split_axis=0, concat_axis=0, tiled=True)


def taken_together(x, axis):
    everything = sent_to_all(x, axis)
    return jnp.sum(everything, axis=0)


def in_order(blocks, dim):
    blocks = jnp.moveaxis(blocks, 0, dim)
    dims = blocks.shape
    return blocks.reshape(*dims[:dim], dims[dim] * dims[dim + 1], *dims[dim + 2 :])


def collect(x, axis, dim):
    return in_order(sent_to_all(x, axis), dim)


def column_taps(padded, cols_out):
    return jnp.concatenate(
        [padded[:, col_tap : col_tap + cols_out] for col_tap in range(3)], axis=-1
    )


def conv_tile(padded, weights):
    rows_out = padded.shape[0] - 2
    cols_out = padded.shape[1] - 2
    stacked = column_taps(padded, cols_out)
    summed = None
    for row_tap in range(3):
        part = jnp.dot(
            stacked[row_tap : row_tap + rows_out],
            weights[row_tap].reshape(-1, weights.shape[3]),
            preferred_element_type=jnp.float32,
        )
        summed = part if summed is None else summed + part
    return summed


def weight_terms(padded, gradient):
    rows_out, cols_out, channels = gradient.shape
    stacked = column_taps(padded, cols_out)
    taps = [
        lax.dot_general(
            stacked[row_tap : row_tap + rows_out],
            gradient,
            (((0, 1), (0, 1)), ((), ())),
            preferred_element_type=jnp.float32,
        )
        for row_tap in range(3)
    ]
    return jnp.stack(taps).reshape(3, 3, padded.shape[2], channels)


def with_partner(x):
    return lax.ppermute(x, "core", [(0, 1), (1, 0)])


def reduced_everywhere(terms):
    core = lax.axis_index("core")
    half = terms.shape[0] // 2
    mine = lax.dynamic_slice_in_dim(terms, core * half, half, 0)
    other = lax.dynamic_slice_in_dim(terms, (1 - core) * half, half, 0)
    chip_sum = mine + with_partner(other)
    portion = sent_and_summed(chip_sum, "lon_chip", 0)
    portion = taken_together(portion, "lat")
    gathered = collect(portion, "lon_chip", 0)
    partner = with_partner(gathered)
    return jnp.where(core == 0, gathered, partner), jnp.where(core == 0, partner, gathered)


def shards(latent_frame, weights_in, weights_out, cotangent):
    tile_rows = latent_frame.shape[0]
    channels = latent_frame.shape[2]
    stacked = jnp.stack([latent_frame, cotangent])
    margin = 2
    widened = with_halo(stacked, ((LON, 2),), margin, True)
    extended = with_halo(widened, (("lat", 1),), margin, False)
    input_pad = extended[0]
    grad_pad = extended[1][1:-1, 1:-1]
    preact_wide = conv_tile(input_pad, weights_in)
    hidden_wide = jax.nn.silu(preact_wide).astype(jnp.bfloat16)
    global_row = lax.axis_index("lat") * tile_rows - 1 + jnp.arange(tile_rows + 2, dtype=jnp.int32)
    inside = (global_row >= 0) & (global_row < tile_rows * lax.axis_size("lat"))
    hidden_pad = jnp.where(inside[:, None, None], hidden_wide, jnp.zeros_like(hidden_wide))
    preact = preact_wide[1:-1, 1:-1]
    input_use = input_pad[1:-1, 1:-1]
    decoded = conv_tile(hidden_pad, weights_out).astype(jnp.bfloat16)
    term_out = weight_terms(hidden_pad, cotangent)
    flipped = jnp.transpose(weights_out[::-1, ::-1], (0, 1, 3, 2))
    grad_hidden = conv_tile(grad_pad, flipped)
    sigmoid_pre = jax.nn.sigmoid(preact)
    grad_pre = (grad_hidden * (sigmoid_pre * (1.0 + preact * (1.0 - sigmoid_pre)))).astype(
        jnp.bfloat16
    )
    grad_pre = lax.optimization_barrier(grad_pre)
    term_in = weight_terms(input_use, grad_pre)
    all_terms = jnp.concatenate(
        [term_in.reshape(9 * channels, channels), term_out.reshape(9 * channels, channels)], axis=0
    )
    grad_in, grad_out = reduced_everywhere(all_terms)
    grad_in = grad_in.reshape(3, 3, channels, channels)
    grad_out = grad_out.reshape(3, 3, channels, channels)
    return (decoded, grad_in, grad_out)


def solution(mesh):
    n_lon, n_lat = mesh.shape["lon"], mesh.shape["lat"]
    split = Mesh(mesh.devices.reshape(n_lon // 2, 2, n_lat), (*LON, "lat"))
    tiled = P("lat", LON, None)
    return jax.shard_map(
        shards,
        mesh=split,
        in_specs=(tiled, P(), P(), tiled),
        out_specs=(tiled, P(), P()),
        check_vma=False,
    )
```

```python
import jax
import jax.numpy as jnp
from jax import lax
from jax.sharding import Mesh, PartitionSpec as P

LON = ("lon_chip", "core")
LAT = ("lat_z", "lat_pair")


def with_halo(block, sides, width, periodic):
    for axis, dim in sides:
        count = lax.axis_size(axis)
        forward = [(i, i + 1) for i in range(count - 1)]
        if periodic:
            forward.append((count - 1, 0))
        backward = [(target, source) for source, target in forward]
        low = lax.ppermute(
            lax.slice_in_dim(block, block.shape[dim] - width, None, axis=dim), axis, forward
        )
        high = lax.ppermute(lax.slice_in_dim(block, 0, width, axis=dim), axis, backward)
        block = jnp.concatenate([low, block, high], axis=dim)
    return block


def in_blocks(x, dim, devices):
    dims = x.shape
    blocks = x.reshape(*dims[:dim], devices, dims[dim] // devices, *dims[dim + 1 :])
    return jnp.moveaxis(blocks, dim, 0)


def sent_and_summed(x, axis, dim):
    blocks = in_blocks(x, dim, lax.axis_size(axis))
    arrived = lax.all_to_all(blocks, axis, split_axis=0, concat_axis=0, tiled=True)
    return arrived.sum(axis=0)


def sent_to_all(x, axis):
    copies = jnp.broadcast_to(x, (lax.axis_size(axis), *x.shape))
    return lax.all_to_all(copies, axis, split_axis=0, concat_axis=0, tiled=True)


def taken_together(x, axis):
    everything = sent_to_all(x, axis)
    return jnp.sum(everything, axis=0)


def in_order(blocks, dim):
    blocks = jnp.moveaxis(blocks, 0, dim)
    dims = blocks.shape
    return blocks.reshape(*dims[:dim], dims[dim] * dims[dim + 1], *dims[dim + 2 :])


def collect(x, axis, dim):
    return in_order(sent_to_all(x, axis), dim)


def column_taps(padded, cols_out):
    return jnp.concatenate(
        [padded[:, col_tap : col_tap + cols_out] for col_tap in range(3)], axis=-1
    )


def conv_tile(padded, weights):
    rows_out = padded.shape[0] - 2
    cols_out = padded.shape[1] - 2
    stacked = column_taps(padded, cols_out)
    summed = None
    for row_tap in range(3):
        part = jnp.dot(
            stacked[row_tap : row_tap + rows_out],
            weights[row_tap].reshape(-1, weights.shape[3]),
            preferred_element_type=jnp.float32,
        )
        summed = part if summed is None else summed + part
    return summed


def weight_terms(padded, gradient):
    rows_out, cols_out, channels = gradient.shape
    stacked = column_taps(padded, cols_out)
    taps = [
        lax.dot_general(
            stacked[row_tap : row_tap + rows_out],
            gradient,
            (((0, 1), (0, 1)), ((), ())),
            preferred_element_type=jnp.float32,
        )
        for row_tap in range(3)
    ]
    return jnp.stack(taps).reshape(3, 3, padded.shape[2], channels)


def with_partner(x):
    return lax.ppermute(x, "core", [(0, 1), (1, 0)])


def reduced_everywhere(terms, decoded):
    core = lax.axis_index("core")
    half = terms.shape[0] // 2
    mine = lax.dynamic_slice_in_dim(terms, core * half, half, 0)
    other = lax.dynamic_slice_in_dim(terms, (1 - core) * half, half, 0)
    received, decoded = lax.optimization_barrier((with_partner(other), decoded))
    chip_sum = mine + received
    portion = sent_and_summed(chip_sum, "lon_chip", 0)
    portion = portion + lax.ppermute(portion, "lat_pair", [(0, 1), (1, 0)])
    portion = taken_together(portion, "lat_z")
    gathered = collect(portion, "lon_chip", 0)
    partner = with_partner(gathered)
    return (
        decoded,
        jnp.where(core == 0, gathered, partner),
        jnp.where(core == 0, partner, gathered),
    )


def shards(latent_frame, weights_in, weights_out, cotangent):
    tile_rows = latent_frame.shape[0]
    channels = latent_frame.shape[2]
    stacked = jnp.stack([latent_frame, cotangent])
    margin = 2
    widened = with_halo(stacked, ((LON, 2),), margin, True)
    extended = with_halo(widened, ((LAT, 1),), margin, False)
    input_pad = extended[0]
    grad_pad = extended[1][1:-1, 1:-1]
    preact_wide = conv_tile(input_pad, weights_in)
    hidden_wide = jax.nn.silu(preact_wide).astype(jnp.bfloat16)
    global_row = lax.axis_index(LAT) * tile_rows - 1 + jnp.arange(tile_rows + 2, dtype=jnp.int32)
    inside = (global_row >= 0) & (global_row < tile_rows * lax.axis_size(LAT))
    hidden_pad = jnp.where(inside[:, None, None], hidden_wide, jnp.zeros_like(hidden_wide))
    preact = preact_wide[1:-1, 1:-1]
    input_use = input_pad[1:-1, 1:-1]
    decoded = conv_tile(hidden_pad, weights_out).astype(jnp.bfloat16)
    term_out = weight_terms(hidden_pad, cotangent)
    flipped = jnp.transpose(weights_out[::-1, ::-1], (0, 1, 3, 2))
    grad_hidden = conv_tile(grad_pad, flipped)
    sigmoid_pre = jax.nn.sigmoid(preact)
    grad_pre = (grad_hidden * (sigmoid_pre * (1.0 + preact * (1.0 - sigmoid_pre)))).astype(
        jnp.bfloat16
    )
    grad_pre = lax.optimization_barrier(grad_pre)
    term_in = weight_terms(input_use, grad_pre)
    all_terms = jnp.concatenate(
        [term_in.reshape(9 * channels, channels), term_out.reshape(9 * channels, channels)], axis=0
    )
    decoded, grad_in, grad_out = reduced_everywhere(all_terms, decoded)
    grad_in = grad_in.reshape(3, 3, channels, channels)
    grad_out = grad_out.reshape(3, 3, channels, channels)
    return (decoded, grad_in, grad_out)


def solution(mesh):
    n_lon, n_lat = mesh.shape["lon"], mesh.shape["lat"]
    split = Mesh(mesh.devices.reshape(n_lon // 2, 2, n_lat // 2, 2), (*LON, *LAT))
    tiled = P(LAT, LON, None)
    return jax.shard_map(
        shards,
        mesh=split,
        in_specs=(tiled, P(), P(), tiled),
        out_specs=(tiled, P(), P()),
        check_vma=False,
    )
```

```python
import jax
import jax.numpy as jnp
from jax import lax
from jax.sharding import Mesh, PartitionSpec as P

LON = ("lon_chip", "core")
LAT = ("lat_z", "lat_pair")


def with_halo(block, sides, width, periodic):
    for axis, dim in sides:
        count = lax.axis_size(axis)
        forward = [(i, i + 1) for i in range(count - 1)]
        if periodic:
            forward.append((count - 1, 0))
        backward = [(target, source) for source, target in forward]
        low = lax.ppermute(
            lax.slice_in_dim(block, block.shape[dim] - width, None, axis=dim), axis, forward
        )
        high = lax.ppermute(lax.slice_in_dim(block, 0, width, axis=dim), axis, backward)
        block = jnp.concatenate([low, block, high], axis=dim)
    return block


def in_blocks(x, dim, devices):
    dims = x.shape
    blocks = x.reshape(*dims[:dim], devices, dims[dim] // devices, *dims[dim + 1 :])
    return jnp.moveaxis(blocks, dim, 0)


def sent_and_summed(x, axis, dim):
    blocks = in_blocks(x, dim, lax.axis_size(axis))
    arrived = lax.all_to_all(blocks, axis, split_axis=0, concat_axis=0, tiled=True)
    return arrived.sum(axis=0)


def sent_to_all(x, axis):
    copies = jnp.broadcast_to(x, (lax.axis_size(axis), *x.shape))
    return lax.all_to_all(copies, axis, split_axis=0, concat_axis=0, tiled=True)


def taken_together(x, axis):
    everything = sent_to_all(x, axis)
    return jnp.sum(everything, axis=0)


def in_order(blocks, dim):
    blocks = jnp.moveaxis(blocks, 0, dim)
    dims = blocks.shape
    return blocks.reshape(*dims[:dim], dims[dim] * dims[dim + 1], *dims[dim + 2 :])


def collect(x, axis, dim):
    return in_order(sent_to_all(x, axis), dim)


def column_taps(padded, cols_out):
    return jnp.concatenate(
        [padded[:, col_tap : col_tap + cols_out] for col_tap in range(3)], axis=-1
    )


def conv_tile(padded, weights):
    rows_out = padded.shape[0] - 2
    cols_out = padded.shape[1] - 2
    stacked = column_taps(padded, cols_out)
    summed = None
    for row_tap in range(3):
        part = jnp.dot(
            stacked[row_tap : row_tap + rows_out],
            weights[row_tap].reshape(-1, weights.shape[3]),
            preferred_element_type=jnp.float32,
        )
        summed = part if summed is None else summed + part
    return summed


def weight_terms(padded, gradient):
    rows_out, cols_out, channels = gradient.shape
    stacked = column_taps(padded, cols_out)
    taps = [
        lax.dot_general(
            stacked[row_tap : row_tap + rows_out],
            gradient,
            (((0, 1), (0, 1)), ((), ())),
            preferred_element_type=jnp.float32,
        )
        for row_tap in range(3)
    ]
    return jnp.stack(taps).reshape(3, 3, padded.shape[2], channels)


def with_partner(x):
    return lax.ppermute(x, "core", [(0, 1), (1, 0)])


def reduced_everywhere(terms, decoded):
    core = lax.axis_index("core")
    half = terms.shape[0] // 2
    mine = lax.dynamic_slice_in_dim(terms, core * half, half, 0)
    other = lax.dynamic_slice_in_dim(terms, (1 - core) * half, half, 0)
    received, decoded = lax.optimization_barrier((with_partner(other), decoded))
    chip_sum = mine + received
    spread = ("lon_chip", "lat_pair")
    portion = sent_and_summed(chip_sum, spread, 0)
    portion = taken_together(portion, "lat_z")
    gathered = collect(portion, spread, 0)
    partner = with_partner(gathered)
    return (
        decoded,
        jnp.where(core == 0, gathered, partner),
        jnp.where(core == 0, partner, gathered),
    )


def shards(latent_frame, weights_in, weights_out, cotangent):
    tile_rows = latent_frame.shape[0]
    channels = latent_frame.shape[2]
    stacked = jnp.stack([latent_frame, cotangent])
    margin = 2
    widened = with_halo(stacked, ((LON, 2),), margin, True)
    extended = with_halo(widened, ((LAT, 1),), margin, False)
    input_pad = extended[0]
    grad_pad = extended[1][1:-1, 1:-1]
    preact_wide = conv_tile(input_pad, weights_in)
    hidden_wide = jax.nn.silu(preact_wide).astype(jnp.bfloat16)
    global_row = lax.axis_index(LAT) * tile_rows - 1 + jnp.arange(tile_rows + 2, dtype=jnp.int32)
    inside = (global_row >= 0) & (global_row < tile_rows * lax.axis_size(LAT))
    hidden_pad = jnp.where(inside[:, None, None], hidden_wide, jnp.zeros_like(hidden_wide))
    preact = preact_wide[1:-1, 1:-1]
    input_use = input_pad[1:-1, 1:-1]
    decoded = conv_tile(hidden_pad, weights_out).astype(jnp.bfloat16)
    term_out = weight_terms(hidden_pad, cotangent)
    flipped = jnp.transpose(weights_out[::-1, ::-1], (0, 1, 3, 2))
    grad_hidden = conv_tile(grad_pad, flipped)
    sigmoid_pre = jax.nn.sigmoid(preact)
    grad_pre = (grad_hidden * (sigmoid_pre * (1.0 + preact * (1.0 - sigmoid_pre)))).astype(
        jnp.bfloat16
    )
    grad_pre = lax.optimization_barrier(grad_pre)
    term_in = weight_terms(input_use, grad_pre)
    all_terms = jnp.concatenate(
        [term_in.reshape(9 * channels, channels), term_out.reshape(9 * channels, channels)], axis=0
    )
    decoded, grad_in, grad_out = reduced_everywhere(all_terms, decoded)
    grad_in = grad_in.reshape(3, 3, channels, channels)
    grad_out = grad_out.reshape(3, 3, channels, channels)
    return (decoded, grad_in, grad_out)


def solution(mesh):
    n_lon, n_lat = mesh.shape["lon"], mesh.shape["lat"]
    split = Mesh(mesh.devices.reshape(n_lon // 2, 2, n_lat // 2, 2), (*LON, *LAT))
    tiled = P(LAT, LON, None)
    return jax.shard_map(
        shards,
        mesh=split,
        in_specs=(tiled, P(), P(), tiled),
        out_specs=(tiled, P(), P()),
        check_vma=False,
    )
```

```python
import jax
import jax.numpy as jnp
from jax import lax
from jax.sharding import Mesh, PartitionSpec as P

LON = ("lon_chip", "core")
LAT = ("lat_z", "lat_pair")


def with_halo(block, sides, width, periodic):
    for axis, dim in sides:
        count = lax.axis_size(axis)
        forward = [(i, i + 1) for i in range(count - 1)]
        if periodic:
            forward.append((count - 1, 0))
        backward = [(target, source) for source, target in forward]
        low = lax.ppermute(
            lax.slice_in_dim(block, block.shape[dim] - width, None, axis=dim), axis, forward
        )
        high = lax.ppermute(lax.slice_in_dim(block, 0, width, axis=dim), axis, backward)
        block = jnp.concatenate([low, block, high], axis=dim)
    return block


def in_blocks(x, dim, devices):
    dims = x.shape
    blocks = x.reshape(*dims[:dim], devices, dims[dim] // devices, *dims[dim + 1 :])
    return jnp.moveaxis(blocks, dim, 0)


def sent_and_summed(x, axis, dim):
    blocks = in_blocks(x, dim, lax.axis_size(axis))
    arrived = lax.all_to_all(blocks, axis, split_axis=0, concat_axis=0, tiled=True)
    return arrived.sum(axis=0)


def sent_to_all(x, axis):
    copies = jnp.broadcast_to(x, (lax.axis_size(axis), *x.shape))
    return lax.all_to_all(copies, axis, split_axis=0, concat_axis=0, tiled=True)


def taken_together(x, axis):
    everything = sent_to_all(x, axis)
    return jnp.sum(everything, axis=0)


def in_order(blocks, dim):
    blocks = jnp.moveaxis(blocks, 0, dim)
    dims = blocks.shape
    return blocks.reshape(*dims[:dim], dims[dim] * dims[dim + 1], *dims[dim + 2 :])


def collect(x, axis, dim):
    return in_order(sent_to_all(x, axis), dim)


def column_taps(padded, cols_out):
    return jnp.concatenate(
        [lax.slice_in_dim(padded, col_tap, col_tap + cols_out, axis=-2) for col_tap in range(3)],
        axis=-1,
    )


def paired_conv(padded, weights):
    rows_out = padded.shape[1] - 2
    cols_out = padded.shape[2] - 2
    stacked = column_taps(padded, cols_out)
    summed = None
    for row_tap in range(3):
        part = lax.dot_general(
            stacked[:, row_tap : row_tap + rows_out],
            weights[:, row_tap].reshape(weights.shape[0], -1, weights.shape[4]),
            (((3,), (1,)), ((0,), (0,))),
            preferred_element_type=jnp.float32,
        )
        summed = part if summed is None else summed + part
    return summed


def paired_weight_terms(padded, gradient):
    pairs, rows_out, cols_out, channels = gradient.shape
    stacked = column_taps(padded, cols_out)
    taps = [
        lax.dot_general(
            stacked[:, row_tap : row_tap + rows_out],
            gradient,
            (((1, 2), (1, 2)), ((0,), (0,))),
            preferred_element_type=jnp.float32,
        )
        for row_tap in range(3)
    ]
    return jnp.stack(taps, axis=1).reshape(pairs * 9 * padded.shape[3], channels)


def conv_tile(padded, weights):
    rows_out = padded.shape[0] - 2
    cols_out = padded.shape[1] - 2
    stacked = column_taps(padded, cols_out)
    summed = None
    for row_tap in range(3):
        part = jnp.dot(
            stacked[row_tap : row_tap + rows_out],
            weights[row_tap].reshape(-1, weights.shape[3]),
            preferred_element_type=jnp.float32,
        )
        summed = part if summed is None else summed + part
    return summed


def with_partner(x):
    return lax.ppermute(x, "core", [(0, 1), (1, 0)])


def reduced_everywhere(terms, decoded):
    core = lax.axis_index("core")
    half = terms.shape[0] // 2
    mine = lax.dynamic_slice_in_dim(terms, core * half, half, 0)
    other = lax.dynamic_slice_in_dim(terms, (1 - core) * half, half, 0)
    received, decoded = lax.optimization_barrier((with_partner(other), decoded))
    chip_sum = mine + received
    spread = ("lon_chip", "lat_pair")
    portion = sent_and_summed(chip_sum, spread, 0)
    portion = taken_together(portion, "lat_z")
    gathered = collect(portion, spread, 0)
    partner = with_partner(gathered)
    return (
        decoded,
        jnp.where(core == 0, gathered, partner),
        jnp.where(core == 0, partner, gathered),
    )


def shards(latent_frame, weights_in, weights_out, cotangent):
    tile_rows = latent_frame.shape[0]
    channels = latent_frame.shape[2]
    stacked = jnp.stack([latent_frame, cotangent])
    margin = 2
    widened = with_halo(stacked, ((LON, 2),), margin, True)
    extended = with_halo(widened, ((LAT, 1),), margin, False)
    flipped = jnp.transpose(weights_out[::-1, ::-1], (0, 1, 3, 2))
    wide = paired_conv(extended, jnp.stack([weights_in, flipped]))
    preact_wide = wide[0]
    grad_hidden = wide[1][1:-1, 1:-1]
    hidden_wide = jax.nn.silu(preact_wide).astype(jnp.bfloat16)
    global_row = lax.axis_index(LAT) * tile_rows - 1 + jnp.arange(tile_rows + 2, dtype=jnp.int32)
    inside = (global_row >= 0) & (global_row < tile_rows * lax.axis_size(LAT))
    hidden_pad = jnp.where(inside[:, None, None], hidden_wide, jnp.zeros_like(hidden_wide))
    preact = preact_wide[1:-1, 1:-1]
    input_use = extended[0][1:-1, 1:-1]
    decoded = conv_tile(hidden_pad, weights_out).astype(jnp.bfloat16)
    sigmoid_pre = jax.nn.sigmoid(preact)
    grad_pre = (grad_hidden * (sigmoid_pre * (1.0 + preact * (1.0 - sigmoid_pre)))).astype(
        jnp.bfloat16
    )
    grad_pre = lax.optimization_barrier(grad_pre)
    all_terms = paired_weight_terms(
        jnp.stack([input_use, hidden_pad]), jnp.stack([grad_pre, cotangent])
    )
    decoded, grad_in, grad_out = reduced_everywhere(all_terms, decoded)
    grad_in = grad_in.reshape(3, 3, channels, channels)
    grad_out = grad_out.reshape(3, 3, channels, channels)
    return (decoded, grad_in, grad_out)


def solution(mesh):
    n_lon, n_lat = mesh.shape["lon"], mesh.shape["lat"]
    split = Mesh(mesh.devices.reshape(n_lon // 2, 2, n_lat // 2, 2), (*LON, *LAT))
    tiled = P(LAT, LON, None)
    return jax.shard_map(
        shards,
        mesh=split,
        in_specs=(tiled, P(), P(), tiled),
        out_specs=(tiled, P(), P()),
        check_vma=False,
    )
```

```python
import jax
import jax.numpy as jnp
from jax import lax
from jax.sharding import Mesh, PartitionSpec as P

LON = ("lon_chip", "core")
LAT = ("lat_z", "lat_pair")


def with_halo(block, sides, width, periodic):
    for axis, dim in sides:
        count = lax.axis_size(axis)
        forward = [(i, i + 1) for i in range(count - 1)]
        if periodic:
            forward.append((count - 1, 0))
        backward = [(target, source) for source, target in forward]
        low = lax.ppermute(
            lax.slice_in_dim(block, block.shape[dim] - width, None, axis=dim), axis, forward
        )
        high = lax.ppermute(lax.slice_in_dim(block, 0, width, axis=dim), axis, backward)
        block = jnp.concatenate([low, block, high], axis=dim)
    return block


def in_blocks(x, dim, devices):
    dims = x.shape
    blocks = x.reshape(*dims[:dim], devices, dims[dim] // devices, *dims[dim + 1 :])
    return jnp.moveaxis(blocks, dim, 0)


def sent_and_summed(x, axis, dim):
    blocks = in_blocks(x, dim, lax.axis_size(axis))
    arrived = lax.all_to_all(blocks, axis, split_axis=0, concat_axis=0, tiled=True)
    return arrived.sum(axis=0)


def sent_to_all(x, axis):
    copies = jnp.broadcast_to(x, (lax.axis_size(axis), *x.shape))
    return lax.all_to_all(copies, axis, split_axis=0, concat_axis=0, tiled=True)


def taken_together(x, axis):
    everything = sent_to_all(x, axis)
    return jnp.sum(everything, axis=0)


def in_order(blocks, dim):
    blocks = jnp.moveaxis(blocks, 0, dim)
    dims = blocks.shape
    return blocks.reshape(*dims[:dim], dims[dim] * dims[dim + 1], *dims[dim + 2 :])


def collect(x, axis, dim):
    return in_order(sent_to_all(x, axis), dim)


def column_taps(padded, cols_out):
    return jnp.concatenate(
        [padded[:, col_tap : col_tap + cols_out] for col_tap in range(3)], axis=-1
    )


def conv_tile(padded, weights):
    rows_out = padded.shape[0] - 2
    cols_out = padded.shape[1] - 2
    stacked = column_taps(padded, cols_out)
    summed = None
    for row_tap in range(3):
        part = jnp.dot(
            stacked[row_tap : row_tap + rows_out],
            weights[row_tap].reshape(-1, weights.shape[3]),
            preferred_element_type=jnp.float32,
        )
        summed = part if summed is None else summed + part
    return summed


def weight_terms(padded, gradient):
    rows_out, cols_out, channels = gradient.shape
    stacked = column_taps(padded, cols_out)
    taps = [
        lax.dot_general(
            stacked[row_tap : row_tap + rows_out],
            gradient,
            (((0, 1), (0, 1)), ((), ())),
            preferred_element_type=jnp.float32,
        )
        for row_tap in range(3)
    ]
    return jnp.stack(taps).reshape(3, 3, padded.shape[2], channels)


def with_partner(x):
    return lax.ppermute(x, "core", [(0, 1), (1, 0)])


def reduced_everywhere(terms, decoded):
    core = lax.axis_index("core")
    half = terms.shape[0] // 2
    mine = lax.dynamic_slice_in_dim(terms, core * half, half, 0)
    other = lax.dynamic_slice_in_dim(terms, (1 - core) * half, half, 0)
    received, decoded = lax.optimization_barrier((with_partner(other), decoded))
    chip_sum = mine + received
    spread = ("lon_chip", "lat_pair")
    portion = sent_and_summed(chip_sum, spread, 0)
    portion = taken_together(portion, "lat_z")
    gathered = collect(portion, spread, 0)
    partner = with_partner(gathered)
    return (
        decoded,
        jnp.where(core == 0, gathered, partner),
        jnp.where(core == 0, partner, gathered),
    )


def shards(latent_frame, weights_in, weights_out, cotangent):
    tile_rows = latent_frame.shape[0]
    channels = latent_frame.shape[2]
    stacked = jnp.stack([latent_frame, cotangent])
    margin = 2
    widened = with_halo(stacked, ((LAT, 1),), margin, False)
    extended = with_halo(widened, ((LON, 2),), margin, True)
    input_pad = extended[0]
    grad_pad = extended[1][1:-1, 1:-1]
    preact_wide = conv_tile(input_pad, weights_in)
    hidden_wide = jax.nn.silu(preact_wide).astype(jnp.bfloat16)
    global_row = lax.axis_index(LAT) * tile_rows - 1 + jnp.arange(tile_rows + 2, dtype=jnp.int32)
    inside = (global_row >= 0) & (global_row < tile_rows * lax.axis_size(LAT))
    hidden_pad = jnp.where(inside[:, None, None], hidden_wide, jnp.zeros_like(hidden_wide))
    preact = preact_wide[1:-1, 1:-1]
    input_use = input_pad[1:-1, 1:-1]
    decoded = conv_tile(hidden_pad, weights_out).astype(jnp.bfloat16)
    term_out = weight_terms(hidden_pad, cotangent)
    flipped = jnp.transpose(weights_out[::-1, ::-1], (0, 1, 3, 2))
    grad_hidden = conv_tile(grad_pad, flipped)
    sigmoid_pre = jax.nn.sigmoid(preact)
    grad_pre = (grad_hidden * (sigmoid_pre * (1.0 + preact * (1.0 - sigmoid_pre)))).astype(
        jnp.bfloat16
    )
    grad_pre = lax.optimization_barrier(grad_pre)
    term_in = weight_terms(input_use, grad_pre)
    all_terms = jnp.concatenate(
        [term_in.reshape(9 * channels, channels), term_out.reshape(9 * channels, channels)], axis=0
    )
    decoded, grad_in, grad_out = reduced_everywhere(all_terms, decoded)
    grad_in = grad_in.reshape(3, 3, channels, channels)
    grad_out = grad_out.reshape(3, 3, channels, channels)
    return (decoded, grad_in, grad_out)


def solution(mesh):
    n_lon, n_lat = mesh.shape["lon"], mesh.shape["lat"]
    split = Mesh(mesh.devices.reshape(n_lon // 2, 2, n_lat // 2, 2), (*LON, *LAT))
    tiled = P(LAT, LON, None)
    return jax.shard_map(
        shards,
        mesh=split,
        in_specs=(tiled, P(), P(), tiled),
        out_specs=(tiled, P(), P()),
        check_vma=False,
    )
```

```python
import jax
import jax.numpy as jnp
from jax import lax
from jax.sharding import Mesh, PartitionSpec as P

LON = ("lon_chip", "core")
LAT = ("lat_z", "lat_pair")


def with_halo(block, sides, width, periodic):
    for axis, dim in sides:
        count = lax.axis_size(axis)
        forward = [(i, i + 1) for i in range(count - 1)]
        if periodic:
            forward.append((count - 1, 0))
        backward = [(target, source) for source, target in forward]
        low = lax.ppermute(
            lax.slice_in_dim(block, block.shape[dim] - width, None, axis=dim), axis, forward
        )
        high = lax.ppermute(lax.slice_in_dim(block, 0, width, axis=dim), axis, backward)
        block = jnp.concatenate([low, block, high], axis=dim)
    return block


def in_blocks(x, dim, devices):
    dims = x.shape
    blocks = x.reshape(*dims[:dim], devices, dims[dim] // devices, *dims[dim + 1 :])
    return jnp.moveaxis(blocks, dim, 0)


def sent_and_summed(x, axis, dim):
    blocks = in_blocks(x, dim, lax.axis_size(axis))
    arrived = lax.all_to_all(blocks, axis, split_axis=0, concat_axis=0, tiled=True)
    return arrived.sum(axis=0)


def sent_to_all(x, axis):
    copies = jnp.broadcast_to(x, (lax.axis_size(axis), *x.shape))
    return lax.all_to_all(copies, axis, split_axis=0, concat_axis=0, tiled=True)


def taken_together(x, axis):
    everything = sent_to_all(x, axis)
    return jnp.sum(everything, axis=0)


def in_order(blocks, dim):
    blocks = jnp.moveaxis(blocks, 0, dim)
    dims = blocks.shape
    return blocks.reshape(*dims[:dim], dims[dim] * dims[dim + 1], *dims[dim + 2 :])


def collect(x, axis, dim):
    return in_order(sent_to_all(x, axis), dim)


def column_taps(padded, cols_out):
    return jnp.concatenate(
        [padded[:, col_tap : col_tap + cols_out] for col_tap in range(3)], axis=-1
    )


def conv_tile(padded, weights):
    rows_out = padded.shape[0] - 2
    cols_out = padded.shape[1] - 2
    stacked = column_taps(padded, cols_out)
    summed = None
    for row_tap in range(3):
        part = jnp.dot(
            stacked[row_tap : row_tap + rows_out],
            weights[row_tap].reshape(-1, weights.shape[3]),
            preferred_element_type=jnp.float32,
        )
        summed = part if summed is None else summed + part
    return summed


def weight_terms(padded, gradient):
    rows_out, cols_out, channels = gradient.shape
    stacked = column_taps(padded, cols_out)
    taps = [
        lax.dot_general(
            stacked[row_tap : row_tap + rows_out],
            gradient,
            (((0, 1), (0, 1)), ((), ())),
            preferred_element_type=jnp.float32,
        )
        for row_tap in range(3)
    ]
    return jnp.stack(taps).reshape(3, 3, padded.shape[2], channels)


def with_partner(x):
    return lax.ppermute(x, "core", [(0, 1), (1, 0)])


def reduced_everywhere(terms, decoded):
    core = lax.axis_index("core")
    half = terms.shape[0] // 2
    mine = lax.dynamic_slice_in_dim(terms, core * half, half, 0)
    other = lax.dynamic_slice_in_dim(terms, (1 - core) * half, half, 0)
    received, decoded = lax.optimization_barrier((with_partner(other), decoded))
    chip_sum = mine + received
    spread = ("lon_chip", "lat_pair")
    portion = sent_and_summed(chip_sum, spread, 0)
    portion = taken_together(portion, "lat_z").astype(jnp.bfloat16)
    gathered = collect(portion, spread, 0)
    partner = with_partner(gathered)
    return (
        decoded,
        jnp.where(core == 0, gathered, partner).astype(jnp.float32),
        jnp.where(core == 0, partner, gathered).astype(jnp.float32),
    )


def shards(latent_frame, weights_in, weights_out, cotangent):
    tile_rows = latent_frame.shape[0]
    channels = latent_frame.shape[2]
    stacked = jnp.stack([latent_frame, cotangent])
    margin = 2
    widened = with_halo(stacked, ((LON, 2),), margin, True)
    extended = with_halo(widened, ((LAT, 1),), margin, False)
    input_pad = extended[0]
    grad_pad = extended[1][1:-1, 1:-1]
    preact_wide = conv_tile(input_pad, weights_in)
    hidden_wide = jax.nn.silu(preact_wide).astype(jnp.bfloat16)
    global_row = lax.axis_index(LAT) * tile_rows - 1 + jnp.arange(tile_rows + 2, dtype=jnp.int32)
    inside = (global_row >= 0) & (global_row < tile_rows * lax.axis_size(LAT))
    hidden_pad = jnp.where(inside[:, None, None], hidden_wide, jnp.zeros_like(hidden_wide))
    preact = preact_wide[1:-1, 1:-1]
    input_use = input_pad[1:-1, 1:-1]
    decoded = conv_tile(hidden_pad, weights_out).astype(jnp.bfloat16)
    term_out = weight_terms(hidden_pad, cotangent)
    flipped = jnp.transpose(weights_out[::-1, ::-1], (0, 1, 3, 2))
    grad_hidden = conv_tile(grad_pad, flipped)
    sigmoid_pre = jax.nn.sigmoid(preact)
    grad_pre = (grad_hidden * (sigmoid_pre * (1.0 + preact * (1.0 - sigmoid_pre)))).astype(
        jnp.bfloat16
    )
    grad_pre = lax.optimization_barrier(grad_pre)
    term_in = weight_terms(input_use, grad_pre)
    all_terms = jnp.concatenate(
        [term_in.reshape(9 * channels, channels), term_out.reshape(9 * channels, channels)], axis=0
    )
    decoded, grad_in, grad_out = reduced_everywhere(all_terms, decoded)
    grad_in = grad_in.reshape(3, 3, channels, channels)
    grad_out = grad_out.reshape(3, 3, channels, channels)
    return (decoded, grad_in, grad_out)


def solution(mesh):
    n_lon, n_lat = mesh.shape["lon"], mesh.shape["lat"]
    split = Mesh(mesh.devices.reshape(n_lon // 2, 2, n_lat // 2, 2), (*LON, *LAT))
    tiled = P(LAT, LON, None)
    return jax.shard_map(
        shards,
        mesh=split,
        in_specs=(tiled, P(), P(), tiled),
        out_specs=(tiled, P(), P()),
        check_vma=False,
    )
```

```python
import jax
import jax.numpy as jnp
from jax import lax
from jax.sharding import Mesh, PartitionSpec as P

LON = ("lon_chip", "core")
LAT = ("lat_z", "lat_pair")


def with_halo(block, sides, width, periodic):
    for axis, dim in sides:
        count = lax.axis_size(axis)
        forward = [(i, i + 1) for i in range(count - 1)]
        if periodic:
            forward.append((count - 1, 0))
        backward = [(target, source) for source, target in forward]
        low = lax.ppermute(
            lax.slice_in_dim(block, block.shape[dim] - width, None, axis=dim), axis, forward
        )
        high = lax.ppermute(lax.slice_in_dim(block, 0, width, axis=dim), axis, backward)
        block = jnp.concatenate([low, block, high], axis=dim)
    return block


def in_blocks(x, dim, devices):
    dims = x.shape
    blocks = x.reshape(*dims[:dim], devices, dims[dim] // devices, *dims[dim + 1 :])
    return jnp.moveaxis(blocks, dim, 0)


def sent_and_summed(x, axis, dim):
    blocks = in_blocks(x, dim, lax.axis_size(axis))
    arrived = lax.all_to_all(blocks, axis, split_axis=0, concat_axis=0, tiled=True)
    return arrived.sum(axis=0)


def sent_to_all(x, axis):
    copies = jnp.broadcast_to(x, (lax.axis_size(axis), *x.shape))
    return lax.all_to_all(copies, axis, split_axis=0, concat_axis=0, tiled=True)


def taken_together(x, axis):
    everything = sent_to_all(x, axis)
    return jnp.sum(everything, axis=0)


def in_order(blocks, dim):
    blocks = jnp.moveaxis(blocks, 0, dim)
    dims = blocks.shape
    return blocks.reshape(*dims[:dim], dims[dim] * dims[dim + 1], *dims[dim + 2 :])


def collect(x, axis, dim):
    return in_order(sent_to_all(x, axis), dim)


def column_taps(padded, cols_out):
    return jnp.concatenate(
        [padded[:, col_tap : col_tap + cols_out] for col_tap in range(3)], axis=-1
    )


def conv_tile(padded, weights):
    rows_out = padded.shape[0] - 2
    cols_out = padded.shape[1] - 2
    stacked = column_taps(padded, cols_out)
    summed = None
    for row_tap in range(3):
        part = jnp.dot(
            stacked[row_tap : row_tap + rows_out],
            weights[row_tap].reshape(-1, weights.shape[3]),
            preferred_element_type=jnp.float32,
        )
        summed = part if summed is None else summed + part
    return summed


def weight_terms(padded, gradient):
    rows_out, cols_out, channels = gradient.shape
    stacked = column_taps(padded, cols_out)
    taps = [
        lax.dot_general(
            stacked[row_tap : row_tap + rows_out],
            gradient,
            (((0, 1), (0, 1)), ((), ())),
            preferred_element_type=jnp.float32,
        )
        for row_tap in range(3)
    ]
    return jnp.stack(taps).reshape(3, 3, padded.shape[2], channels)


def with_partner(x):
    return lax.ppermute(x, "core", [(0, 1), (1, 0)])


def reduced_everywhere(terms, decoded):
    core = lax.axis_index("core")
    half = terms.shape[0] // 2
    mine = lax.dynamic_slice_in_dim(terms, core * half, half, 0)
    other = lax.dynamic_slice_in_dim(terms, (1 - core) * half, half, 0)
    received, decoded = lax.optimization_barrier((with_partner(other), decoded))
    chip_sum = mine + received
    spread = ("lon_chip", "lat_pair")
    portion = sent_and_summed(chip_sum, spread, 0)
    portion = taken_together(portion, "lat_z").astype(jnp.bfloat16)
    gathered = collect(portion, spread, 0)
    slots = jnp.zeros((2, *gathered.shape), jnp.float32)
    slots = lax.dynamic_update_slice_in_dim(slots, gathered.astype(jnp.float32)[None], core, 0)
    partner = with_partner(gathered)
    slots = lax.dynamic_update_slice_in_dim(slots, partner.astype(jnp.float32)[None], 1 - core, 0)
    return decoded, slots[0], slots[1]


def shards(latent_frame, weights_in, weights_out, cotangent):
    tile_rows = latent_frame.shape[0]
    channels = latent_frame.shape[2]
    stacked = jnp.stack([latent_frame, cotangent])
    margin = 2
    widened = with_halo(stacked, ((LON, 2),), margin, True)
    extended = with_halo(widened, ((LAT, 1),), margin, False)
    input_pad = extended[0]
    grad_pad = extended[1][1:-1, 1:-1]
    preact_wide = conv_tile(input_pad, weights_in)
    hidden_wide = jax.nn.silu(preact_wide).astype(jnp.bfloat16)
    global_row = lax.axis_index(LAT) * tile_rows - 1 + jnp.arange(tile_rows + 2, dtype=jnp.int32)
    inside = (global_row >= 0) & (global_row < tile_rows * lax.axis_size(LAT))
    hidden_pad = jnp.where(inside[:, None, None], hidden_wide, jnp.zeros_like(hidden_wide))
    preact = preact_wide[1:-1, 1:-1]
    input_use = input_pad[1:-1, 1:-1]
    decoded = conv_tile(hidden_pad, weights_out).astype(jnp.bfloat16)
    term_out = weight_terms(hidden_pad, cotangent)
    flipped = jnp.transpose(weights_out[::-1, ::-1], (0, 1, 3, 2))
    grad_hidden = conv_tile(grad_pad, flipped)
    sigmoid_pre = jax.nn.sigmoid(preact)
    grad_pre = (grad_hidden * (sigmoid_pre * (1.0 + preact * (1.0 - sigmoid_pre)))).astype(
        jnp.bfloat16
    )
    grad_pre = lax.optimization_barrier(grad_pre)
    term_in = weight_terms(input_use, grad_pre)
    all_terms = jnp.concatenate(
        [term_in.reshape(9 * channels, channels), term_out.reshape(9 * channels, channels)], axis=0
    )
    decoded, grad_in, grad_out = reduced_everywhere(all_terms, decoded)
    grad_in = grad_in.reshape(3, 3, channels, channels)
    grad_out = grad_out.reshape(3, 3, channels, channels)
    return (decoded, grad_in, grad_out)


def solution(mesh):
    n_lon, n_lat = mesh.shape["lon"], mesh.shape["lat"]
    split = Mesh(mesh.devices.reshape(n_lon // 2, 2, n_lat // 2, 2), (*LON, *LAT))
    tiled = P(LAT, LON, None)
    return jax.shard_map(
        shards,
        mesh=split,
        in_specs=(tiled, P(), P(), tiled),
        out_specs=(tiled, P(), P()),
        check_vma=False,
    )
```

```python
import jax
import jax.numpy as jnp
from jax import lax
from jax.sharding import Mesh, PartitionSpec as P

LON = ("lon_chip", "core")
LAT = ("lat_z", "lat_pair")


def with_halo(block, sides, width, periodic):
    for axis, dim in sides:
        count = lax.axis_size(axis)
        forward = [(i, i + 1) for i in range(count - 1)]
        if periodic:
            forward.append((count - 1, 0))
        backward = [(target, source) for source, target in forward]
        low = lax.ppermute(
            lax.slice_in_dim(block, block.shape[dim] - width, None, axis=dim), axis, forward
        )
        high = lax.ppermute(lax.slice_in_dim(block, 0, width, axis=dim), axis, backward)
        block = jnp.concatenate([low, block, high], axis=dim)
    return block


def in_blocks(x, dim, devices):
    dims = x.shape
    blocks = x.reshape(*dims[:dim], devices, dims[dim] // devices, *dims[dim + 1 :])
    return jnp.moveaxis(blocks, dim, 0)


def sent_and_summed(x, axis, dim):
    blocks = in_blocks(x, dim, lax.axis_size(axis))
    arrived = lax.all_to_all(blocks, axis, split_axis=0, concat_axis=0, tiled=True)
    return arrived.sum(axis=0)


def sent_to_all(x, axis):
    copies = jnp.broadcast_to(x, (lax.axis_size(axis), *x.shape))
    return lax.all_to_all(copies, axis, split_axis=0, concat_axis=0, tiled=True)


def taken_together(x, axis):
    everything = sent_to_all(x, axis)
    return jnp.sum(everything, axis=0)


def in_order(blocks, dim):
    blocks = jnp.moveaxis(blocks, 0, dim)
    dims = blocks.shape
    return blocks.reshape(*dims[:dim], dims[dim] * dims[dim + 1], *dims[dim + 2 :])


def collect(x, axis, dim):
    return in_order(sent_to_all(x, axis), dim)


def column_taps(padded, cols_out):
    return jnp.concatenate(
        [padded[:, col_tap : col_tap + cols_out] for col_tap in range(3)], axis=-1
    )


def conv_tile(padded, weights):
    rows_out = padded.shape[0] - 2
    cols_out = padded.shape[1] - 2
    channels, width = weights.shape[2], weights.shape[3]
    stacked = column_taps(padded, cols_out)
    merged = jnp.transpose(weights, (1, 2, 0, 3)).reshape(3 * channels, 3 * width)
    spread = jnp.dot(stacked, merged, preferred_element_type=jnp.float32)
    summed = None
    for row_tap in range(3):
        part = spread[row_tap : row_tap + rows_out, :, row_tap * width : (row_tap + 1) * width]
        summed = part if summed is None else summed + part
    return summed


def weight_terms(padded, gradient):
    rows_out, cols_out, channels = gradient.shape
    stacked = column_taps(padded, cols_out)
    shifted = jnp.concatenate(
        [jnp.pad(gradient, ((row_tap, 2 - row_tap), (0, 0), (0, 0))) for row_tap in range(3)],
        axis=-1,
    )
    terms = lax.dot_general(
        stacked, shifted, (((0, 1), (0, 1)), ((), ())), preferred_element_type=jnp.float32
    )
    terms = terms.reshape(3, padded.shape[2], 3, channels)
    return jnp.transpose(terms, (2, 0, 1, 3))


def with_partner(x):
    return lax.ppermute(x, "core", [(0, 1), (1, 0)])


def reduced_everywhere(terms, decoded):
    core = lax.axis_index("core")
    half = terms.shape[0] // 2
    mine = lax.dynamic_slice_in_dim(terms, core * half, half, 0)
    other = lax.dynamic_slice_in_dim(terms, (1 - core) * half, half, 0)
    received, decoded = lax.optimization_barrier((with_partner(other), decoded))
    chip_sum = mine + received
    spread = ("lon_chip", "lat_pair")
    portion = sent_and_summed(chip_sum, spread, 0)
    portion = taken_together(portion, "lat_z").astype(jnp.bfloat16)
    gathered = collect(portion, spread, 0)
    slots = jnp.zeros((2, *gathered.shape), jnp.float32)
    slots = lax.dynamic_update_slice_in_dim(slots, gathered.astype(jnp.float32)[None], core, 0)
    partner = with_partner(gathered)
    slots = lax.dynamic_update_slice_in_dim(slots, partner.astype(jnp.float32)[None], 1 - core, 0)
    return decoded, slots[0], slots[1]


def shards(latent_frame, weights_in, weights_out, cotangent):
    tile_rows = latent_frame.shape[0]
    channels = latent_frame.shape[2]
    stacked = jnp.stack([latent_frame, cotangent])
    margin = 2
    widened = with_halo(stacked, ((LON, 2),), margin, True)
    extended = with_halo(widened, ((LAT, 1),), margin, False)
    input_pad = extended[0]
    grad_pad = extended[1][1:-1, 1:-1]
    preact_wide = conv_tile(input_pad, weights_in)
    hidden_wide = jax.nn.silu(preact_wide).astype(jnp.bfloat16)
    global_row = lax.axis_index(LAT) * tile_rows - 1 + jnp.arange(tile_rows + 2, dtype=jnp.int32)
    inside = (global_row >= 0) & (global_row < tile_rows * lax.axis_size(LAT))
    hidden_pad = jnp.where(inside[:, None, None], hidden_wide, jnp.zeros_like(hidden_wide))
    preact = preact_wide[1:-1, 1:-1]
    input_use = input_pad[1:-1, 1:-1]
    decoded = conv_tile(hidden_pad, weights_out).astype(jnp.bfloat16)
    term_out = weight_terms(hidden_pad, cotangent)
    flipped = jnp.transpose(weights_out[::-1, ::-1], (0, 1, 3, 2))
    grad_hidden = conv_tile(grad_pad, flipped)
    sigmoid_pre = jax.nn.sigmoid(preact)
    grad_pre = (grad_hidden * (sigmoid_pre * (1.0 + preact * (1.0 - sigmoid_pre)))).astype(
        jnp.bfloat16
    )
    grad_pre = lax.optimization_barrier(grad_pre)
    term_in = weight_terms(input_use, grad_pre)
    all_terms = jnp.concatenate(
        [term_in.reshape(9 * channels, channels), term_out.reshape(9 * channels, channels)], axis=0
    )
    decoded, grad_in, grad_out = reduced_everywhere(all_terms, decoded)
    grad_in = grad_in.reshape(3, 3, channels, channels)
    grad_out = grad_out.reshape(3, 3, channels, channels)
    return (decoded, grad_in, grad_out)


def solution(mesh):
    n_lon, n_lat = mesh.shape["lon"], mesh.shape["lat"]
    split = Mesh(mesh.devices.reshape(n_lon // 2, 2, n_lat // 2, 2), (*LON, *LAT))
    tiled = P(LAT, LON, None)
    return jax.shard_map(
        shards,
        mesh=split,
        in_specs=(tiled, P(), P(), tiled),
        out_specs=(tiled, P(), P()),
        check_vma=False,
    )
```

```python
import jax
import jax.numpy as jnp
from jax import lax
from jax.sharding import Mesh, PartitionSpec as P

LON = ("lon_chip", "core")
LAT = ("lat_z", "lat_pair")


def with_halo(block, sides, width, periodic):
    for axis, dim in sides:
        count = lax.axis_size(axis)
        forward = [(i, i + 1) for i in range(count - 1)]
        if periodic:
            forward.append((count - 1, 0))
        backward = [(target, source) for source, target in forward]
        low = lax.ppermute(
            lax.slice_in_dim(block, block.shape[dim] - width, None, axis=dim), axis, forward
        )
        high = lax.ppermute(lax.slice_in_dim(block, 0, width, axis=dim), axis, backward)
        block = jnp.concatenate([low, block, high], axis=dim)
    return block


def in_blocks(x, dim, devices):
    dims = x.shape
    blocks = x.reshape(*dims[:dim], devices, dims[dim] // devices, *dims[dim + 1 :])
    return jnp.moveaxis(blocks, dim, 0)


def sent_and_summed(x, axis, dim):
    blocks = in_blocks(x, dim, lax.axis_size(axis))
    arrived = lax.all_to_all(blocks, axis, split_axis=0, concat_axis=0, tiled=True)
    return arrived.sum(axis=0)


def sent_to_all(x, axis):
    copies = jnp.broadcast_to(x, (lax.axis_size(axis), *x.shape))
    return lax.all_to_all(copies, axis, split_axis=0, concat_axis=0, tiled=True)


def taken_together(x, axis):
    everything = sent_to_all(x, axis)
    return jnp.sum(everything, axis=0)


def in_order(blocks, dim):
    blocks = jnp.moveaxis(blocks, 0, dim)
    dims = blocks.shape
    return blocks.reshape(*dims[:dim], dims[dim] * dims[dim + 1], *dims[dim + 2 :])


def collect(x, axis, dim):
    return in_order(sent_to_all(x, axis), dim)


def column_taps(padded, cols_out):
    return jnp.concatenate(
        [padded[:, col_tap : col_tap + cols_out] for col_tap in range(3)], axis=-1
    )


def conv_tile(padded, weights):
    rows_out = padded.shape[0] - 2
    cols_out = padded.shape[1] - 2
    stacked = column_taps(padded, cols_out)
    summed = None
    for row_tap in range(3):
        part = jnp.dot(
            stacked[row_tap : row_tap + rows_out],
            weights[row_tap].reshape(-1, weights.shape[3]),
            preferred_element_type=jnp.float32,
        )
        summed = part if summed is None else summed + part
    return summed


def merged_conv(padded, weights):
    rows_out = padded.shape[0] - 2
    cols_out = padded.shape[1] - 2
    channels, width = weights.shape[2], weights.shape[3]
    stacked = column_taps(padded, cols_out)
    merged = jnp.transpose(weights, (1, 2, 0, 3)).reshape(3 * channels, 3 * width)
    spread = jnp.dot(stacked, merged, preferred_element_type=jnp.float32)
    summed = None
    for row_tap in range(3):
        part = spread[row_tap : row_tap + rows_out, :, row_tap * width : (row_tap + 1) * width]
        summed = part if summed is None else summed + part
    return summed


def weight_terms(padded, gradient):
    rows_out, cols_out, channels = gradient.shape
    stacked = column_taps(padded, cols_out)
    taps = [
        lax.dot_general(
            stacked[row_tap : row_tap + rows_out],
            gradient,
            (((0, 1), (0, 1)), ((), ())),
            preferred_element_type=jnp.float32,
        )
        for row_tap in range(3)
    ]
    return jnp.stack(taps).reshape(3, 3, padded.shape[2], channels)


def with_partner(x):
    return lax.ppermute(x, "core", [(0, 1), (1, 0)])


def reduced_everywhere(terms, decoded):
    core = lax.axis_index("core")
    half = terms.shape[0] // 2
    mine = lax.dynamic_slice_in_dim(terms, core * half, half, 0)
    other = lax.dynamic_slice_in_dim(terms, (1 - core) * half, half, 0)
    received, decoded = lax.optimization_barrier((with_partner(other), decoded))
    chip_sum = mine + received
    spread = ("lon_chip", "lat_pair")
    portion = sent_and_summed(chip_sum, spread, 0)
    portion = taken_together(portion, "lat_z").astype(jnp.bfloat16)
    gathered = collect(portion, spread, 0)
    slots = jnp.zeros((2, *gathered.shape), jnp.float32)
    slots = lax.dynamic_update_slice_in_dim(slots, gathered.astype(jnp.float32)[None], core, 0)
    partner = with_partner(gathered)
    slots = lax.dynamic_update_slice_in_dim(slots, partner.astype(jnp.float32)[None], 1 - core, 0)
    return decoded, slots[0], slots[1]


def shards(latent_frame, weights_in, weights_out, cotangent):
    tile_rows = latent_frame.shape[0]
    channels = latent_frame.shape[2]
    stacked = jnp.stack([latent_frame, cotangent])
    margin = 2
    widened = with_halo(stacked, ((LON, 2),), margin, True)
    extended = with_halo(widened, ((LAT, 1),), margin, False)
    input_pad = extended[0]
    grad_pad = extended[1][1:-1, 1:-1]
    preact_wide = merged_conv(input_pad, weights_in)
    hidden_wide = jax.nn.silu(preact_wide).astype(jnp.bfloat16)
    global_row = lax.axis_index(LAT) * tile_rows - 1 + jnp.arange(tile_rows + 2, dtype=jnp.int32)
    inside = (global_row >= 0) & (global_row < tile_rows * lax.axis_size(LAT))
    hidden_pad = jnp.where(inside[:, None, None], hidden_wide, jnp.zeros_like(hidden_wide))
    preact = preact_wide[1:-1, 1:-1]
    input_use = input_pad[1:-1, 1:-1]
    decoded = conv_tile(hidden_pad, weights_out).astype(jnp.bfloat16)
    term_out = weight_terms(hidden_pad, cotangent)
    flipped = jnp.transpose(weights_out[::-1, ::-1], (0, 1, 3, 2))
    grad_hidden = merged_conv(grad_pad, flipped)
    sigmoid_pre = jax.nn.sigmoid(preact)
    grad_pre = (grad_hidden * (sigmoid_pre * (1.0 + preact * (1.0 - sigmoid_pre)))).astype(
        jnp.bfloat16
    )
    grad_pre = lax.optimization_barrier(grad_pre)
    term_in = weight_terms(input_use, grad_pre)
    all_terms = jnp.concatenate(
        [term_in.reshape(9 * channels, channels), term_out.reshape(9 * channels, channels)], axis=0
    )
    decoded, grad_in, grad_out = reduced_everywhere(all_terms, decoded)
    grad_in = grad_in.reshape(3, 3, channels, channels)
    grad_out = grad_out.reshape(3, 3, channels, channels)
    return (decoded, grad_in, grad_out)


def solution(mesh):
    n_lon, n_lat = mesh.shape["lon"], mesh.shape["lat"]
    split = Mesh(mesh.devices.reshape(n_lon // 2, 2, n_lat // 2, 2), (*LON, *LAT))
    tiled = P(LAT, LON, None)
    return jax.shard_map(
        shards,
        mesh=split,
        in_specs=(tiled, P(), P(), tiled),
        out_specs=(tiled, P(), P()),
        check_vma=False,
    )
```

```python
import jax
import jax.numpy as jnp
from jax import lax
from jax.sharding import Mesh, PartitionSpec as P

LON = ("lon_chip", "core")
LAT = ("lat_z", "lat_pair")


def with_halo(block, sides, width, periodic):
    for axis, dim in sides:
        count = lax.axis_size(axis)
        forward = [(i, i + 1) for i in range(count - 1)]
        if periodic:
            forward.append((count - 1, 0))
        backward = [(target, source) for source, target in forward]
        low = lax.ppermute(
            lax.slice_in_dim(block, block.shape[dim] - width, None, axis=dim), axis, forward
        )
        high = lax.ppermute(lax.slice_in_dim(block, 0, width, axis=dim), axis, backward)
        block = jnp.concatenate([low, block, high], axis=dim)
    return block


def in_blocks(x, dim, devices):
    dims = x.shape
    blocks = x.reshape(*dims[:dim], devices, dims[dim] // devices, *dims[dim + 1 :])
    return jnp.moveaxis(blocks, dim, 0)


def sent_and_summed(x, axis, dim):
    blocks = in_blocks(x, dim, lax.axis_size(axis))
    arrived = lax.all_to_all(blocks, axis, split_axis=0, concat_axis=0, tiled=True)
    return arrived.sum(axis=0)


def sent_to_all(x, axis):
    copies = jnp.broadcast_to(x, (lax.axis_size(axis), *x.shape))
    return lax.all_to_all(copies, axis, split_axis=0, concat_axis=0, tiled=True)


def taken_together(x, axis):
    everything = sent_to_all(x, axis)
    return jnp.sum(everything, axis=0)


def in_order(blocks, dim):
    blocks = jnp.moveaxis(blocks, 0, dim)
    dims = blocks.shape
    return blocks.reshape(*dims[:dim], dims[dim] * dims[dim + 1], *dims[dim + 2 :])


def collect(x, axis, dim):
    return in_order(sent_to_all(x, axis), dim)


def column_taps(padded, cols_out):
    return jnp.concatenate(
        [padded[:, col_tap : col_tap + cols_out] for col_tap in range(3)], axis=-1
    )


def conv_tile(padded, weights):
    rows_out = padded.shape[0] - 2
    cols_out = padded.shape[1] - 2
    stacked = column_taps(padded, cols_out)
    summed = None
    for row_tap in range(3):
        part = jnp.dot(
            stacked[row_tap : row_tap + rows_out],
            weights[row_tap].reshape(-1, weights.shape[3]),
            preferred_element_type=jnp.float32,
        )
        summed = part if summed is None else summed + part
    return summed


def merged_conv(padded, weights):
    rows_out = padded.shape[0] - 2
    cols_out = padded.shape[1] - 2
    channels, width = weights.shape[2], weights.shape[3]
    stacked = column_taps(padded, cols_out)
    merged = jnp.transpose(weights, (1, 2, 0, 3)).reshape(3 * channels, 3 * width)
    spread = jnp.dot(stacked, merged, preferred_element_type=jnp.float32)
    summed = None
    for row_tap in range(3):
        part = spread[row_tap : row_tap + rows_out, :, row_tap * width : (row_tap + 1) * width]
        summed = part if summed is None else summed + part
    return summed


def weight_terms(padded, gradient):
    rows_out, cols_out, channels = gradient.shape
    stacked = column_taps(padded, cols_out)
    shifted = jnp.concatenate(
        [jnp.pad(gradient, ((row_tap, 2 - row_tap), (0, 0), (0, 0))) for row_tap in range(3)],
        axis=-1,
    )
    terms = lax.dot_general(
        stacked, shifted, (((0, 1), (0, 1)), ((), ())), preferred_element_type=jnp.float32
    )
    return terms.reshape(-1, channels)


def tap_order(terms, channels):
    return jnp.transpose(terms.reshape(3, channels, 3, channels), (2, 0, 1, 3))


def with_partner(x):
    return lax.ppermute(x, "core", [(0, 1), (1, 0)])


def reduced_everywhere(terms, decoded):
    core = lax.axis_index("core")
    half = terms.shape[0] // 2
    mine = lax.dynamic_slice_in_dim(terms, core * half, half, 0)
    other = lax.dynamic_slice_in_dim(terms, (1 - core) * half, half, 0)
    received, decoded = lax.optimization_barrier((with_partner(other), decoded))
    chip_sum = mine + received
    spread = ("lon_chip", "lat_pair")
    portion = sent_and_summed(chip_sum, spread, 0)
    portion = taken_together(portion, "lat_z").astype(jnp.bfloat16)
    gathered = collect(portion, spread, 0)
    slots = jnp.zeros((2, *gathered.shape), jnp.float32)
    slots = lax.dynamic_update_slice_in_dim(slots, gathered.astype(jnp.float32)[None], core, 0)
    partner = with_partner(gathered)
    slots = lax.dynamic_update_slice_in_dim(slots, partner.astype(jnp.float32)[None], 1 - core, 0)
    return decoded, slots[0], slots[1]


def shards(latent_frame, weights_in, weights_out, cotangent):
    tile_rows = latent_frame.shape[0]
    channels = latent_frame.shape[2]
    stacked = jnp.stack([latent_frame, cotangent])
    margin = 2
    widened = with_halo(stacked, ((LON, 2),), margin, True)
    extended = with_halo(widened, ((LAT, 1),), margin, False)
    input_pad = extended[0]
    grad_pad = extended[1][1:-1, 1:-1]
    preact_wide = merged_conv(input_pad, weights_in)
    hidden_wide = jax.nn.silu(preact_wide).astype(jnp.bfloat16)
    global_row = lax.axis_index(LAT) * tile_rows - 1 + jnp.arange(tile_rows + 2, dtype=jnp.int32)
    inside = (global_row >= 0) & (global_row < tile_rows * lax.axis_size(LAT))
    hidden_pad = jnp.where(inside[:, None, None], hidden_wide, jnp.zeros_like(hidden_wide))
    preact = preact_wide[1:-1, 1:-1]
    input_use = input_pad[1:-1, 1:-1]
    decoded = conv_tile(hidden_pad, weights_out).astype(jnp.bfloat16)
    term_out = weight_terms(hidden_pad, cotangent)
    flipped = jnp.transpose(weights_out[::-1, ::-1], (0, 1, 3, 2))
    grad_hidden = merged_conv(grad_pad, flipped)
    sigmoid_pre = jax.nn.sigmoid(preact)
    grad_pre = (grad_hidden * (sigmoid_pre * (1.0 + preact * (1.0 - sigmoid_pre)))).astype(
        jnp.bfloat16
    )
    grad_pre = lax.optimization_barrier(grad_pre)
    term_in = weight_terms(input_use, grad_pre)
    all_terms = jnp.concatenate([term_in, term_out], axis=0)
    decoded, grad_in, grad_out = reduced_everywhere(all_terms, decoded)
    grad_in = tap_order(grad_in, channels)
    grad_out = tap_order(grad_out, channels)
    return (decoded, grad_in, grad_out)


def solution(mesh):
    n_lon, n_lat = mesh.shape["lon"], mesh.shape["lat"]
    split = Mesh(mesh.devices.reshape(n_lon // 2, 2, n_lat // 2, 2), (*LON, *LAT))
    tiled = P(LAT, LON, None)
    return jax.shard_map(
        shards,
        mesh=split,
        in_specs=(tiled, P(), P(), tiled),
        out_specs=(tiled, P(), P()),
        check_vma=False,
    )
```

```python
import jax
import jax.numpy as jnp
from jax import lax
from jax.sharding import Mesh, PartitionSpec as P

LON = ("lon_chip", "core")
LAT = ("lat_z", "lat_pair")


def with_halo(block, sides, width, periodic):
    for axis, dim in sides:
        count = lax.axis_size(axis)
        forward = [(i, i + 1) for i in range(count - 1)]
        if periodic:
            forward.append((count - 1, 0))
        backward = [(target, source) for source, target in forward]
        low = lax.ppermute(
            lax.slice_in_dim(block, block.shape[dim] - width, None, axis=dim), axis, forward
        )
        high = lax.ppermute(lax.slice_in_dim(block, 0, width, axis=dim), axis, backward)
        block = jnp.concatenate([low, block, high], axis=dim)
    return block


def in_blocks(x, dim, devices):
    dims = x.shape
    blocks = x.reshape(*dims[:dim], devices, dims[dim] // devices, *dims[dim + 1 :])
    return jnp.moveaxis(blocks, dim, 0)


def sent_and_summed(x, axis, dim):
    blocks = in_blocks(x, dim, lax.axis_size(axis))
    arrived = lax.all_to_all(blocks, axis, split_axis=0, concat_axis=0, tiled=True)
    return arrived.sum(axis=0)


def sent_to_all(x, axis):
    copies = jnp.broadcast_to(x, (lax.axis_size(axis), *x.shape))
    return lax.all_to_all(copies, axis, split_axis=0, concat_axis=0, tiled=True)


def taken_together(x, axis):
    everything = sent_to_all(x, axis)
    return jnp.sum(everything, axis=0)


def in_order(blocks, dim):
    blocks = jnp.moveaxis(blocks, 0, dim)
    dims = blocks.shape
    return blocks.reshape(*dims[:dim], dims[dim] * dims[dim + 1], *dims[dim + 2 :])


def collect(x, axis, dim):
    return in_order(sent_to_all(x, axis), dim)


def column_taps(padded, cols_out):
    return jnp.concatenate(
        [padded[:, col_tap : col_tap + cols_out] for col_tap in range(3)], axis=-1
    )


def conv_tile(padded, weights):
    rows_out = padded.shape[0] - 2
    cols_out = padded.shape[1] - 2
    stacked = column_taps(padded, cols_out)
    summed = None
    for row_tap in range(3):
        part = jnp.dot(
            stacked[row_tap : row_tap + rows_out],
            weights[row_tap].reshape(-1, weights.shape[3]),
            preferred_element_type=jnp.float32,
        )
        summed = part if summed is None else summed + part
    return summed


def merged_conv(padded, weights, local=None, edge=0):
    rows_out = padded.shape[0] - 2
    cols_out = padded.shape[1] - 2
    channels, width = weights.shape[2], weights.shape[3]
    merged = jnp.transpose(weights, (1, 2, 0, 3)).reshape(3 * channels, 3 * width)
    if local is None:
        spread = jnp.dot(column_taps(padded, cols_out), merged, preferred_element_type=jnp.float32)
    else:
        inner = jnp.dot(column_taps(local, cols_out), merged, preferred_element_type=jnp.float32)
        rims = jnp.concatenate([padded[:edge], padded[padded.shape[0] - edge :]], axis=0)
        outer = jnp.dot(column_taps(rims, cols_out), merged, preferred_element_type=jnp.float32)
        spread = jnp.concatenate([outer[:edge], inner, outer[edge:]], axis=0)
    summed = None
    for row_tap in range(3):
        part = spread[row_tap : row_tap + rows_out, :, row_tap * width : (row_tap + 1) * width]
        summed = part if summed is None else summed + part
    return summed


def weight_terms(padded, gradient):
    rows_out, cols_out, channels = gradient.shape
    stacked = column_taps(padded, cols_out)
    taps = [
        lax.dot_general(
            stacked[row_tap : row_tap + rows_out],
            gradient,
            (((0, 1), (0, 1)), ((), ())),
            preferred_element_type=jnp.float32,
        )
        for row_tap in range(3)
    ]
    return jnp.stack(taps).reshape(3, 3, padded.shape[2], channels)


def with_partner(x):
    return lax.ppermute(x, "core", [(0, 1), (1, 0)])


def reduced_everywhere(terms, decoded):
    core = lax.axis_index("core")
    half = terms.shape[0] // 2
    mine = lax.dynamic_slice_in_dim(terms, core * half, half, 0)
    other = lax.dynamic_slice_in_dim(terms, (1 - core) * half, half, 0)
    received, decoded = lax.optimization_barrier((with_partner(other), decoded))
    chip_sum = mine + received
    spread = ("lon_chip", "lat_pair")
    portion = sent_and_summed(chip_sum, spread, 0)
    portion = taken_together(portion, "lat_z").astype(jnp.bfloat16)
    gathered = collect(portion, spread, 0)
    slots = jnp.zeros((2, *gathered.shape), jnp.float32)
    slots = lax.dynamic_update_slice_in_dim(slots, gathered.astype(jnp.float32)[None], core, 0)
    partner = with_partner(gathered)
    slots = lax.dynamic_update_slice_in_dim(slots, partner.astype(jnp.float32)[None], 1 - core, 0)
    return decoded, slots[0], slots[1]


def shards(latent_frame, weights_in, weights_out, cotangent):
    tile_rows = latent_frame.shape[0]
    channels = latent_frame.shape[2]
    stacked = jnp.stack([latent_frame, cotangent])
    margin = 2
    widened = with_halo(stacked, ((LON, 2),), margin, True)
    extended = with_halo(widened, ((LAT, 1),), margin, False)
    input_pad = extended[0]
    grad_pad = extended[1][1:-1, 1:-1]
    preact_wide = merged_conv(input_pad, weights_in, widened[0], margin)
    hidden_wide = jax.nn.silu(preact_wide).astype(jnp.bfloat16)
    global_row = lax.axis_index(LAT) * tile_rows - 1 + jnp.arange(tile_rows + 2, dtype=jnp.int32)
    inside = (global_row >= 0) & (global_row < tile_rows * lax.axis_size(LAT))
    hidden_pad = jnp.where(inside[:, None, None], hidden_wide, jnp.zeros_like(hidden_wide))
    preact = preact_wide[1:-1, 1:-1]
    input_use = input_pad[1:-1, 1:-1]
    decoded = conv_tile(hidden_pad, weights_out).astype(jnp.bfloat16)
    term_out = weight_terms(hidden_pad, cotangent)
    flipped = jnp.transpose(weights_out[::-1, ::-1], (0, 1, 3, 2))
    grad_hidden = merged_conv(grad_pad, flipped, widened[1][:, 1:-1], margin - 1)
    sigmoid_pre = jax.nn.sigmoid(preact)
    grad_pre = (grad_hidden * (sigmoid_pre * (1.0 + preact * (1.0 - sigmoid_pre)))).astype(
        jnp.bfloat16
    )
    grad_pre = lax.optimization_barrier(grad_pre)
    term_in = weight_terms(input_use, grad_pre)
    all_terms = jnp.concatenate(
        [term_in.reshape(9 * channels, channels), term_out.reshape(9 * channels, channels)], axis=0
    )
    decoded, grad_in, grad_out = reduced_everywhere(all_terms, decoded)
    grad_in = grad_in.reshape(3, 3, channels, channels)
    grad_out = grad_out.reshape(3, 3, channels, channels)
    return (decoded, grad_in, grad_out)


def solution(mesh):
    n_lon, n_lat = mesh.shape["lon"], mesh.shape["lat"]
    split = Mesh(mesh.devices.reshape(n_lon // 2, 2, n_lat // 2, 2), (*LON, *LAT))
    tiled = P(LAT, LON, None)
    return jax.shard_map(
        shards,
        mesh=split,
        in_specs=(tiled, P(), P(), tiled),
        out_specs=(tiled, P(), P()),
        check_vma=False,
    )
```
